32 devices in a mesh: req: 8 (over y, x, core), head: 4 (over z).
Axes of the slice: x: 2, y: 2, z: 4, core: 2. Of those that a mesh axis runs over, the one named last changes fastest.
Arguments:
- tokens: bfloat16 [4096, 2048], P('req'), may hold values from -6 to 6
- norm_gain: float32 [2048], replicated, may hold values from 0.1 to 1.9
- router_weight: float32 [2048, 8], replicated, may hold values from -0.125 to 0.125
- kv_weight: bfloat16 [2048, 4096], P('req', 'head'), may hold values from -0.125 to 0.125
- query_weight: bfloat16 [8, 2048, 2048], P(None, 'req', 'head'), may hold values from -0.125 to 0.125
- out_weight: bfloat16 [8, 2048, 2048], P(None, 'head', 'req'), may hold values from -0.5 to 0.5
- expert_ids: int32 [4096, 2], P('req'), may hold values from 0 to 7, all different within a row
- lengths: int32 [8], replicated, may hold values from 128 to 2048, as said below
- kv_cache: bfloat16 [8, 16, 2048, 256], P('req', 'head'), may hold values from -320 to 320
Outputs:
- attended: bfloat16 [4096, 2048], P(('req', 'head'))
- new_kv: bfloat16 [8, 16, 512, 256], P('req', 'head')
The draws below stay inside these ranges and needn't reach their ends.
Inputs may be any that keep to these rules, and one draw needn't show every extreme that they name: `lengths`: some request holds exactly 2048 cached positions.
All inputs are finite; a program needn't handle non-finite values.
Results may differ from the reference program's by a relative error of at most 0.012.
The reference program's roundings to bfloat16 on the way count: a program that leaves them out, or rounds other values in their place, can miss the bound.
Values may be sent and summed in bfloat16 or wider, within the bound.
No kernel may reach another device: no remote copies, remote signals or barrier semaphores. Data moves between devices by JAX's collectives and lax.ppermute only.
A program may use at most 128 MiB of HBM per device.

```python
import math
import jax
import jax.numpy as jnp
from jax import lax

D = 2048
HEADS = 16
HD = 128
EXPERTS = 8
TOPK = 2
SPAN = 512
CACHE = 2048
REQUESTS = 8
TOKENS = 4096
N_HEAD = 4


def draw_lengths(key, part):
    first_key, second_key = jax.random.split(key)
    base = jax.random.randint(first_key, (REQUESTS,), CACHE // 16, CACHE // 2 + 1)
    order = jax.random.permutation(second_key, REQUESTS)
    return jnp.where(order < 1 + REQUESTS // 16, CACHE, base).astype(jnp.int32)


def draw_kv_cache(key, part):
    shape = (REQUESTS, HEADS, CACHE, HD)
    key_part, value_part = jax.random.split(key, 2)
    key_rows = 1.5 * jnp.clip(jax.random.normal(key_part, shape, jnp.float32), -6.0, 6.0)
    value_rows = 2.0 * jnp.clip(jax.random.normal(value_part, shape, jnp.float32), -6.0, 6.0)
    return jnp.concatenate([key_rows, value_rows], axis=-1).astype(jnp.bfloat16)


def block_scale(own_key, dims, pieces, low, top_value):
    gain = 1.0
    for position, parts in pieces:
        steps = jax.random.uniform(jax.random.fold_in(jax.random.fold_in(own_key, 6), position), (parts,), jnp.float32, low / len(pieces), top_value / len(pieces))
        gain = gain * jnp.repeat(jnp.exp(steps), dims[position] // parts).reshape((-1,) + (1,) * (len(dims) - 1 - position))
    return gain


def distinct(key, rows, amount, top, lift):
    ranking = jax.random.permutation(jax.random.fold_in(key, 1), amount)
    boost = ranking
    for power in range(3):
        boost = boost * boost // amount
    boost = boost * lift // amount
    tickets = jax.random.randint(jax.random.fold_in(key, 2), (rows, amount), 0, 4096) + boost
    sure = jax.random.permutation(jax.random.fold_in(key, 3), rows)[jnp.arange(amount) % rows]
    tickets = jnp.where(jnp.arange(rows)[:, None] == sure[None, :], 1 << 14, tickets)
    score = tickets * amount + jnp.arange(amount)
    return lax.top_k(score.astype(jnp.int32), top)[1].astype(jnp.int32)


def bell_draw(rng, extent, width, bound, pieces=(), held_as=jnp.bfloat16):
    array = width * jax.random.normal(rng, extent, jnp.float32)
    if pieces:
        array = array * block_scale(rng, extent, pieces, -0.22, 0.18)
    return jnp.clip(array, -bound, bound).astype(held_as)


def setup_inputs(seed: int = 0) -> dict:
    key_list = jax.random.split(jax.random.key(seed), 10)
    tokens = bell_draw(key_list[0], (TOKENS, D), 1.0, 6.0, ((0, 8),))
    norm_gain = jnp.clip(1.0 + 0.18 * jax.random.normal(key_list[1], (D,), jnp.float32), 0.1, 1.9)
    router_weight = bell_draw(key_list[2], (D, EXPERTS), D ** -0.5, 0.125, (), jnp.float32)
    kv_weight = bell_draw(key_list[3], (D, HEADS * 2 * HD), D ** -0.5, 0.125, ((0, 8), (1, 4)))
    query_weight = bell_draw(key_list[4], (EXPERTS, D, HEADS * HD), D ** -0.5, 0.125, ((1, 8), (2, 4)))
    out_weight = bell_draw(key_list[5], (EXPERTS, HEADS * HD, D), HD ** -0.5, 0.5, ((1, 4), (2, 8)))
    expert_ids = distinct(key_list[6], TOKENS, EXPERTS, TOPK, 2048)
    lengths = draw_lengths(jax.random.fold_in(key_list[9], 71), 0)
    kv_cache = draw_kv_cache(jax.random.fold_in(key_list[9], 71), 0)
    return {"tokens": tokens, "norm_gain": norm_gain, "router_weight": router_weight, "kv_weight": kv_weight, "query_weight": query_weight, "out_weight": out_weight, "expert_ids": expert_ids, "lengths": lengths, "kv_cache": kv_cache}


NEG_LARGE = -1e+30
EPSILON = 1e-06

def normalize(tokens, norm_gain):
    widened = tokens.astype(jnp.float32)
    factor = lax.rsqrt(lax.optimization_barrier(jnp.mean(widened * widened, axis=-1, keepdims=True)) + EPSILON)
    return (widened * factor * norm_gain).astype(jnp.bfloat16)

def gate_pair(normed, router_weight, expert_ids):
    logits = jnp.dot(normed.astype(jnp.float32), router_weight, precision=lax.Precision.HIGHEST)
    one_hot = jnp.arange(router_weight.shape[1])[None, None, :] == expert_ids[:, :, None]
    chosen = lax.optimization_barrier(jnp.sum(jnp.where(one_hot, logits[:, None, :], 0.0), axis=-1))
    logit_gap = chosen[:, 1] - chosen[:, 0]
    return jnp.stack([1.0 / (1.0 + jnp.exp(logit_gap)), 1.0 / (1.0 + jnp.exp(-logit_gap))], axis=1)

def rotate(vectors, positions):
    half_dim = vectors.shape[-1] // 2
    inv_freq = jnp.exp(-math.log(10000.0) * jnp.arange(half_dim, dtype=jnp.float32) / half_dim)
    angles = positions[:, None] * inv_freq[None, :]
    cosine_table = jnp.cos(angles)
    sine_table = jnp.sin(angles)
    front_half = vectors[..., :half_dim]
    back_half = vectors[..., half_dim:]
    return jnp.concatenate([front_half * cosine_table - back_half * sine_table, back_half * cosine_table + front_half * sine_table], axis=-1)

def reference(tokens, norm_gain, router_weight, kv_weight, query_weight, out_weight, expert_ids, lengths, kv_cache):
    score_scale = HD ** (-0.5)
    wide_query = query_weight.astype(jnp.float32)
    group_heads = HEADS // N_HEAD
    group_width = group_heads * HD
    grouped_out = out_weight.reshape(EXPERTS, N_HEAD, group_width, D)

    def one_request(request):
        row_block = lax.dynamic_slice_in_dim(tokens, request * SPAN, SPAN, 0)
        token_ids = lax.dynamic_slice_in_dim(expert_ids, request * SPAN, SPAN, 0)
        cached = lax.dynamic_index_in_dim(kv_cache, request, 0, keepdims=False)
        cached_len = lax.dynamic_index_in_dim(lengths, request, 0, keepdims=False)
        normed = normalize(row_block, norm_gain)
        gate_values = gate_pair(normed, router_weight, token_ids)
        projected = jnp.dot(normed, kv_weight, preferred_element_type=jnp.float32).reshape(SPAN, HEADS, 2, HD)
        positions = (cached_len + jnp.arange(SPAN)).astype(jnp.float32)
        new_keys = rotate(jnp.transpose(projected[:, :, 0], (1, 0, 2)), positions)
        new_values = jnp.transpose(projected[:, :, 1], (1, 0, 2))
        fresh_kv = jnp.concatenate([new_keys, new_values], axis=-1).astype(jnp.bfloat16)
        query_all = jnp.einsum('td,edn->ten', normed.astype(jnp.float32), wide_query, precision=lax.Precision.HIGHEST)
        one_hot = jnp.arange(EXPERTS)[None, None, :] == token_ids[:, :, None]
        query_sel = lax.optimization_barrier(jnp.sum(jnp.where(one_hot[..., None], query_all[:, None], 0.0), axis=2))
        queries = jnp.transpose(query_sel.reshape(SPAN * 2, HEADS, HD), (1, 0, 2))
        queries = rotate(queries, jnp.repeat(positions, 2)).astype(jnp.bfloat16)
        row_ids = (jnp.arange(SPAN * 2) // 2)[:, None]
        col_ids = jnp.arange(CACHE + SPAN)[None, :]
        allowed = jnp.where(col_ids < CACHE, col_ids < cached_len, col_ids - CACHE <= row_ids)

        def one_head(operands):
            head_queries, head_cache, head_fresh = operands
            key_rows = jnp.concatenate([head_cache[:, :HD], head_fresh[:, :HD]], axis=0)
            value_rows = jnp.concatenate([head_cache[:, HD:], head_fresh[:, HD:]], axis=0)
            scores = jnp.dot(head_queries, key_rows.T, preferred_element_type=jnp.float32) * score_scale
            scores = jnp.where(allowed, scores, NEG_LARGE)
            row_peak = lax.optimization_barrier(jnp.max(scores, axis=-1, keepdims=True))
            weights = jnp.where(allowed, jnp.exp(scores - row_peak), 0.0)
            summed = jnp.dot(weights.astype(jnp.bfloat16), value_rows, preferred_element_type=jnp.float32)
            return summed / lax.optimization_barrier(jnp.sum(weights, axis=-1, keepdims=True))
        heads_out = lax.map(one_head, (queries, cached, fresh_kv))
        heads_out = jnp.transpose(heads_out, (1, 0, 2)).reshape(SPAN, 2, HEADS * HD)
        weighted = (gate_values[:, :, None] * heads_out).astype(jnp.bfloat16)
        mixture = lax.optimization_barrier(jnp.sum(jnp.where(one_hot[..., None], weighted[:, :, None, :], 0), axis=1))
        mixture = mixture.reshape(SPAN, EXPERTS, N_HEAD, group_width)

        def add_group(group, total):
            group_mix = lax.dynamic_index_in_dim(mixture, group, 2, keepdims=False).reshape(SPAN, EXPERTS * group_width)
            group_weight = lax.dynamic_index_in_dim(grouped_out, group, 1, keepdims=False).reshape(EXPERTS * group_width, D)
            group_part = jnp.dot(group_mix, group_weight, preferred_element_type=jnp.float32).astype(jnp.bfloat16)
            return total + group_part.astype(jnp.float32)
        summed_out = lax.fori_loop(0, N_HEAD, add_group, jnp.zeros((SPAN, D), jnp.float32))
        return (summed_out.astype(jnp.bfloat16), fresh_kv)
    outputs, fresh_all = lax.map(one_request, jnp.arange(REQUESTS))
    return (outputs.reshape(TOKENS, D), fresh_all)
```

```python
import math

import jax
import jax.numpy as jnp
from jax import lax
from jax.sharding import PartitionSpec as P

NEG_LARGE = -1e30
EPSILON = 1e-06


def normalize(tokens, norm_gain):
    widened = tokens.astype(jnp.float32)
    factor = lax.rsqrt(jnp.mean(widened * widened, axis=-1, keepdims=True) + EPSILON)
    return (widened * factor * norm_gain).astype(jnp.bfloat16)


def gate_pair(normed, router_weight, expert_ids):
    logits = jnp.dot(normed.astype(jnp.float32), router_weight, precision=lax.Precision.HIGHEST)
    one_hot = jnp.arange(router_weight.shape[1])[None, None, :] == expert_ids[:, :, None]
    chosen = jnp.sum(jnp.where(one_hot, logits[:, None, :], 0.0), axis=-1)
    logit_gap = chosen[:, 1] - chosen[:, 0]
    return jnp.stack([1.0 / (1.0 + jnp.exp(logit_gap)), 1.0 / (1.0 + jnp.exp(-logit_gap))], axis=1)


def rotate(vectors, positions):
    half_dim = vectors.shape[-1] // 2
    inv_freq = jnp.exp(-math.log(10000.0) * jnp.arange(half_dim, dtype=jnp.float32) / half_dim)
    angles = positions[:, None] * inv_freq[None, :]
    cosine_table = jnp.cos(angles)
    sine_table = jnp.sin(angles)
    front_half = vectors[..., :half_dim]
    back_half = vectors[..., half_dim:]
    return jnp.concatenate(
        [
            front_half * cosine_table - back_half * sine_table,
            back_half * cosine_table + front_half * sine_table,
        ],
        axis=-1,
    )


def pick_length(lengths, wanted):
    return jnp.sum(jnp.where(jnp.arange(lengths.shape[0]) == wanted, lengths, 0))


def absorb(carry_state, queries, key_rows, value_rows, allowed):
    row_peak, row_total, row_accum = carry_state
    scale_factor = queries.shape[-1] ** (-0.5)
    scores = (
        jnp.einsum("hqd,hkd->hqk", queries, key_rows, preferred_element_type=jnp.float32)
        * scale_factor
    )
    scores = jnp.where(allowed[None], scores, NEG_LARGE)
    new_peak = jnp.maximum(row_peak, jnp.max(scores, axis=-1))
    weights = jnp.where(allowed[None], jnp.exp(scores - new_peak[..., None]), 0.0)
    shrink = jnp.exp(row_peak - new_peak)
    row_total = row_total * shrink + jnp.sum(weights, axis=-1)
    row_accum = row_accum * shrink[..., None] + jnp.einsum(
        "hqk,hkd->hqd", weights.astype(jnp.bfloat16), value_rows, preferred_element_type=jnp.float32
    )
    return (new_peak, row_total, row_accum)


def cache_pass(
    queries, source, lowest, highest, first_block, last_block, anchor, block_len, carry_state
):
    head_dim = source.shape[2] // 2

    def block_step(block_id, running):
        block_rows = lax.dynamic_slice_in_dim(source, block_id * block_len, block_len, 1)
        key_index = anchor + block_id * block_len + jnp.arange(block_len)
        allowed = ((key_index >= lowest) & (key_index < highest))[None, :]
        return absorb(
            running, queries, block_rows[..., :head_dim], block_rows[..., head_dim:], allowed
        )

    return lax.fori_loop(
        jnp.asarray(first_block, jnp.int32),
        jnp.asarray(last_block, jnp.int32),
        block_step,
        carry_state,
    )


def chain_reduce(parts, axis):
    count = lax.axis_size(axis)
    me = lax.axis_index(axis)
    blocks = parts.reshape(count, parts.shape[0] // count, parts.shape[1])
    own = lax.dynamic_index_in_dim(blocks, me, 0, keepdims=False).astype(jnp.float32)
    if count == 1:
        return own.astype(parts.dtype)

    def run(step_block, pairs_of):
        received = None
        for step in range(1, count):
            block = lax.dynamic_index_in_dim(
                blocks, jnp.clip(step_block(step), 0, count - 1), 0, keepdims=False
            )
            if received is not None:
                block = (received.astype(jnp.float32) + block.astype(jnp.float32)).astype(
                    parts.dtype
                )
            received = lax.ppermute(block, axis, pairs_of(step))
        return received.astype(jnp.float32)

    rightward = run(
        lambda step: me + count - step,
        lambda step: [(src, src + 1) for src in range(step) if src + 1 < count],
    )
    leftward = run(
        lambda step: me - count + step,
        lambda step: [(src, src - 1) for src in range(count - step, count) if src >= 1],
    )
    return (own + rightward + leftward).astype(parts.dtype)


def shards(
    tokens,
    norm_gain,
    router_weight,
    kv_weight,
    query_weight,
    out_weight,
    expert_ids,
    lengths,
    kv_cache,
):
    normed = normalize(tokens, norm_gain)
    tok_count = normed.shape[0]
    experts = query_weight.shape[0]
    head_dim = kv_cache.shape[3] // 2
    local_heads = query_weight.shape[2] // head_dim
    cache_len = kv_cache.shape[2]
    block_len = min(512, cache_len // 4)
    gate_values = gate_pair(normed, router_weight, expert_ids)
    part_rows = normed
    projected = jnp.dot(
        part_rows,
        lax.all_gather(kv_weight, "req", axis=0, tiled=True),
        preferred_element_type=jnp.float32,
    )
    part_rows = normed
    query_all = jnp.einsum(
        "tc,ecn->ten",
        part_rows,
        lax.all_gather(query_weight, "req", axis=1, tiled=True),
        preferred_element_type=jnp.float32,
    )
    req_index = lax.axis_index("req")
    own_length = pick_length(lengths, req_index)
    positions = (own_length + jnp.arange(tok_count)).astype(jnp.float32)
    projected = projected.reshape(tok_count, local_heads, 2, head_dim)
    new_keys = rotate(jnp.transpose(projected[:, :, 0], (1, 0, 2)), positions)
    new_values = jnp.transpose(projected[:, :, 1], (1, 0, 2))
    fresh_kv = jnp.concatenate([new_keys, new_values], axis=-1).astype(jnp.bfloat16)
    one_hot = jnp.arange(experts)[None, None, :] == expert_ids[:, :, None]
    query_sel = jnp.sum(jnp.where(one_hot[..., None], query_all[:, None], 0.0), axis=2)
    queries = jnp.transpose(query_sel.reshape(tok_count * 2, local_heads, head_dim), (1, 0, 2))
    queries = rotate(queries, jnp.repeat(positions, 2)).astype(jnp.bfloat16)
    own_cache = kv_cache[0]
    query_rows = tok_count * 2
    empty_state = (
        jnp.full((local_heads, query_rows), NEG_LARGE, jnp.float32),
        jnp.zeros((local_heads, query_rows), jnp.float32),
        jnp.zeros((local_heads, query_rows, head_dim), jnp.float32),
    )
    carry_state = cache_pass(
        queries,
        own_cache,
        0,
        own_length,
        0,
        (own_length + block_len - 1) // block_len,
        0,
        block_len,
        empty_state,
    )
    row_ids = jnp.arange(query_rows) // 2
    causal = row_ids[:, None] >= jnp.arange(tok_count)[None, :]
    carry_state = absorb(
        carry_state, queries, fresh_kv[..., :head_dim], fresh_kv[..., head_dim:], causal
    )
    heads_out = carry_state[2] / carry_state[1][..., None]
    heads_out = jnp.transpose(heads_out, (1, 0, 2)).reshape(tok_count, 2, local_heads * head_dim)
    weighted = (gate_values[:, :, None] * heads_out).astype(jnp.bfloat16)
    mixture = jnp.sum(jnp.where(one_hot[..., None], weighted[:, :, None, :], 0), axis=1)
    mixture_flat = mixture.reshape(tok_count, experts * local_heads * head_dim)
    weight_piece = lax.all_gather(out_weight, "req", axis=2, tiled=True)
    flat_piece = weight_piece.reshape(experts * local_heads * head_dim, weight_piece.shape[2])
    partial_value = jnp.dot(mixture_flat, flat_piece, preferred_element_type=jnp.float32)
    result = chain_reduce(partial_value.astype(jnp.bfloat16), "head")
    return (result, fresh_kv[None])


def solution(mesh):
    placed = (
        P("req", None),
        P(),
        P(),
        P("req", "head"),
        P(None, "req", "head"),
        P(None, "head", "req"),
        P("req", None),
        P(),
        P("req", "head", None, None),
    )
    return jax.shard_map(
        shards,
        mesh=mesh,
        in_specs=placed,
        out_specs=(P(("req", "head"), None), P("req", "head", None, None)),
        check_vma=False,
    )
```

```python
import math

import jax
import jax.numpy as jnp
from jax import lax
from jax.sharding import PartitionSpec as P

NEG_LARGE = -1e30
EPSILON = 1e-06


def normalize(tokens, norm_gain):
    widened = tokens.astype(jnp.float32)
    factor = lax.rsqrt(jnp.mean(widened * widened, axis=-1, keepdims=True) + EPSILON)
    return (widened * factor * norm_gain).astype(jnp.bfloat16)


def gate_pair(normed, router_weight, expert_ids):
    logits = jnp.dot(normed.astype(jnp.float32), router_weight, precision=lax.Precision.HIGHEST)
    one_hot = jnp.arange(router_weight.shape[1])[None, None, :] == expert_ids[:, :, None]
    chosen = jnp.sum(jnp.where(one_hot, logits[:, None, :], 0.0), axis=-1)
    logit_gap = chosen[:, 1] - chosen[:, 0]
    return jnp.stack([1.0 / (1.0 + jnp.exp(logit_gap)), 1.0 / (1.0 + jnp.exp(-logit_gap))], axis=1)


def rotate(vectors, positions):
    half_dim = vectors.shape[-1] // 2
    inv_freq = jnp.exp(-math.log(10000.0) * jnp.arange(half_dim, dtype=jnp.float32) / half_dim)
    angles = positions[:, None] * inv_freq[None, :]
    cosine_table = jnp.cos(angles)
    sine_table = jnp.sin(angles)
    front_half = vectors[..., :half_dim]
    back_half = vectors[..., half_dim:]
    return jnp.concatenate(
        [
            front_half * cosine_table - back_half * sine_table,
            back_half * cosine_table + front_half * sine_table,
        ],
        axis=-1,
    )


def pick_length(lengths, wanted):
    return jnp.sum(jnp.where(jnp.arange(lengths.shape[0]) == wanted, lengths, 0))


def absorb(carry_state, queries, key_rows, value_rows, allowed):
    row_peak, row_total, row_accum = carry_state
    scale_factor = queries.shape[-1] ** (-0.5)
    scores = (
        jnp.einsum("hqd,hkd->hqk", queries, key_rows, preferred_element_type=jnp.float32)
        * scale_factor
    )
    scores = jnp.where(allowed[None], scores, NEG_LARGE)
    new_peak = jnp.maximum(row_peak, jnp.max(scores, axis=-1))
    weights = jnp.where(allowed[None], jnp.exp(scores - new_peak[..., None]), 0.0)
    shrink = jnp.exp(row_peak - new_peak)
    row_total = row_total * shrink + jnp.sum(weights, axis=-1)
    row_accum = row_accum * shrink[..., None] + jnp.einsum(
        "hqk,hkd->hqd", weights.astype(jnp.bfloat16), value_rows, preferred_element_type=jnp.float32
    )
    return (new_peak, row_total, row_accum)


def cache_pass(
    queries, source, lowest, highest, first_block, last_block, anchor, block_len, carry_state
):
    head_dim = source.shape[2] // 2

    def block_step(block_id, running):
        block_rows = lax.dynamic_slice_in_dim(source, block_id * block_len, block_len, 1)
        key_index = anchor + block_id * block_len + jnp.arange(block_len)
        allowed = ((key_index >= lowest) & (key_index < highest))[None, :]
        return absorb(
            running, queries, block_rows[..., :head_dim], block_rows[..., head_dim:], allowed
        )

    return lax.fori_loop(
        jnp.asarray(first_block, jnp.int32),
        jnp.asarray(last_block, jnp.int32),
        block_step,
        carry_state,
    )


def chain_reduce(parts, axis):
    count = lax.axis_size(axis)
    me = lax.axis_index(axis)
    blocks = parts.reshape(count, parts.shape[0] // count, parts.shape[1])
    own = lax.dynamic_index_in_dim(blocks, me, 0, keepdims=False).astype(jnp.float32)
    if count == 1:
        return own.astype(parts.dtype)

    def run(step_block, pairs_of):
        received = None
        for step in range(1, count):
            block = lax.dynamic_index_in_dim(
                blocks, jnp.clip(step_block(step), 0, count - 1), 0, keepdims=False
            )
            if received is not None:
                block = (received.astype(jnp.float32) + block.astype(jnp.float32)).astype(
                    parts.dtype
                )
            received = lax.ppermute(block, axis, pairs_of(step))
        return received.astype(jnp.float32)

    rightward = run(
        lambda step: me + count - step,
        lambda step: [(src, src + 1) for src in range(step) if src + 1 < count],
    )
    leftward = run(
        lambda step: me - count + step,
        lambda step: [(src, src - 1) for src in range(count - step, count) if src >= 1],
    )
    return (own + rightward + leftward).astype(parts.dtype)


def shards(
    tokens,
    norm_gain,
    router_weight,
    kv_weight,
    query_weight,
    out_weight,
    expert_ids,
    lengths,
    kv_cache,
):
    normed = normalize(tokens, norm_gain)
    tok_count = normed.shape[0]
    experts = query_weight.shape[0]
    head_dim = kv_cache.shape[3] // 2
    local_heads = query_weight.shape[2] // head_dim
    cache_len = kv_cache.shape[2]
    block_len = min(512, cache_len // 4)
    gate_values = gate_pair(normed, router_weight, expert_ids)
    query_full = lax.all_gather(query_weight, "req", axis=1, tiled=True)
    query_full, kv_weight, out_weight = lax.optimization_barrier(
        (query_full, kv_weight, out_weight)
    )
    kv_full = lax.all_gather(kv_weight, "req", axis=0, tiled=True)
    out_full = lax.all_gather(out_weight, "req", axis=2, tiled=True)
    projected = jnp.dot(normed, kv_full, preferred_element_type=jnp.float32)
    query_all = jnp.einsum(
        "tc,ecn->ten", normed, query_full, preferred_element_type=jnp.float32
    )
    req_index = lax.axis_index("req")
    own_length = pick_length(lengths, req_index)
    positions = (own_length + jnp.arange(tok_count)).astype(jnp.float32)
    projected = projected.reshape(tok_count, local_heads, 2, head_dim)
    new_keys = rotate(jnp.transpose(projected[:, :, 0], (1, 0, 2)), positions)
    new_values = jnp.transpose(projected[:, :, 1], (1, 0, 2))
    fresh_kv = jnp.concatenate([new_keys, new_values], axis=-1).astype(jnp.bfloat16)
    one_hot = jnp.arange(experts)[None, None, :] == expert_ids[:, :, None]
    query_sel = jnp.sum(jnp.where(one_hot[..., None], query_all[:, None], 0.0), axis=2)
    queries = jnp.transpose(query_sel.reshape(tok_count * 2, local_heads, head_dim), (1, 0, 2))
    queries = rotate(queries, jnp.repeat(positions, 2)).astype(jnp.bfloat16)
    own_cache = kv_cache[0]
    query_rows = tok_count * 2
    empty_state = (
        jnp.full((local_heads, query_rows), NEG_LARGE, jnp.float32),
        jnp.zeros((local_heads, query_rows), jnp.float32),
        jnp.zeros((local_heads, query_rows, head_dim), jnp.float32),
    )
    carry_state = cache_pass(
        queries,
        own_cache,
        0,
        own_length,
        0,
        (own_length + block_len - 1) // block_len,
        0,
        block_len,
        empty_state,
    )
    row_ids = jnp.arange(query_rows) // 2
    causal = row_ids[:, None] >= jnp.arange(tok_count)[None, :]
    carry_state = absorb(
        carry_state, queries, fresh_kv[..., :head_dim], fresh_kv[..., head_dim:], causal
    )
    heads_out = carry_state[2] / carry_state[1][..., None]
    heads_out = jnp.transpose(heads_out, (1, 0, 2)).reshape(tok_count, 2, local_heads * head_dim)
    weighted = (gate_values[:, :, None] * heads_out).astype(jnp.bfloat16)
    mixture = jnp.sum(jnp.where(one_hot[..., None], weighted[:, :, None, :], 0), axis=1)
    mixture_flat = mixture.reshape(tok_count, experts * local_heads * head_dim)
    weight_piece = out_full
    flat_piece = weight_piece.reshape(experts * local_heads * head_dim, weight_piece.shape[2])
    partial_value = jnp.dot(mixture_flat, flat_piece, preferred_element_type=jnp.float32)
    result = chain_reduce(partial_value.astype(jnp.bfloat16), "head")
    return (result, fresh_kv[None])


def solution(mesh):
    placed = (
        P("req", None),
        P(),
        P(),
        P("req", "head"),
        P(None, "req", "head"),
        P(None, "head", "req"),
        P("req", None),
        P(),
        P("req", "head", None, None),
    )
    return jax.shard_map(
        shards,
        mesh=mesh,
        in_specs=placed,
        out_specs=(P(("req", "head"), None), P("req", "head", None, None)),
        check_vma=False,
    )
```

```python
import math

import jax
import jax.numpy as jnp
from jax import lax
from jax.sharding import PartitionSpec as P

NEG_LARGE = -1e30
EPSILON = 1e-06


def normalize(tokens, norm_gain):
    widened = tokens.astype(jnp.float32)
    factor = lax.rsqrt(jnp.mean(widened * widened, axis=-1, keepdims=True) + EPSILON)
    return (widened * factor * norm_gain).astype(jnp.bfloat16)


def gate_pair(normed, router_weight, expert_ids):
    logits = jnp.dot(normed.astype(jnp.float32), router_weight, precision=lax.Precision.HIGHEST)
    one_hot = jnp.arange(router_weight.shape[1])[None, None, :] == expert_ids[:, :, None]
    chosen = jnp.sum(jnp.where(one_hot, logits[:, None, :], 0.0), axis=-1)
    logit_gap = chosen[:, 1] - chosen[:, 0]
    return jnp.stack([1.0 / (1.0 + jnp.exp(logit_gap)), 1.0 / (1.0 + jnp.exp(-logit_gap))], axis=1)


def rotate(vectors, positions):
    half_dim = vectors.shape[-1] // 2
    inv_freq = jnp.exp(-math.log(10000.0) * jnp.arange(half_dim, dtype=jnp.float32) / half_dim)
    angles = positions[:, None] * inv_freq[None, :]
    cosine_table = jnp.cos(angles)
    sine_table = jnp.sin(angles)
    front_half = vectors[..., :half_dim]
    back_half = vectors[..., half_dim:]
    return jnp.concatenate(
        [
            front_half * cosine_table - back_half * sine_table,
            back_half * cosine_table + front_half * sine_table,
        ],
        axis=-1,
    )


def pick_length(lengths, wanted):
    return jnp.sum(jnp.where(jnp.arange(lengths.shape[0]) == wanted, lengths, 0))


def absorb(carry_state, queries, key_rows, value_rows, allowed):
    row_peak, row_total, row_accum = carry_state
    scale_factor = queries.shape[-1] ** (-0.5)
    scores = (
        jnp.einsum("hqd,hkd->hqk", queries, key_rows, preferred_element_type=jnp.float32)
        * scale_factor
    )
    scores = jnp.where(allowed[None], scores, NEG_LARGE)
    new_peak = jnp.maximum(row_peak, jnp.max(scores, axis=-1))
    weights = jnp.where(allowed[None], jnp.exp(scores - new_peak[..., None]), 0.0)
    shrink = jnp.exp(row_peak - new_peak)
    row_total = row_total * shrink + jnp.sum(weights, axis=-1)
    row_accum = row_accum * shrink[..., None] + jnp.einsum(
        "hqk,hkd->hqd", weights.astype(jnp.bfloat16), value_rows, preferred_element_type=jnp.float32
    )
    return (new_peak, row_total, row_accum)


def cache_pass(
    queries, source, lowest, highest, first_block, last_block, anchor, block_len, carry_state
):
    head_dim = source.shape[2] // 2

    def block_step(block_id, running):
        block_rows = lax.dynamic_slice_in_dim(source, block_id * block_len, block_len, 1)
        key_index = anchor + block_id * block_len + jnp.arange(block_len)
        allowed = ((key_index >= lowest) & (key_index < highest))[None, :]
        return absorb(
            running, queries, block_rows[..., :head_dim], block_rows[..., head_dim:], allowed
        )

    return lax.fori_loop(
        jnp.asarray(first_block, jnp.int32),
        jnp.asarray(last_block, jnp.int32),
        block_step,
        carry_state,
    )


def chain_reduce(parts, axis):
    count = lax.axis_size(axis)
    me = lax.axis_index(axis)
    blocks = parts.reshape(count, parts.shape[0] // count, parts.shape[1])
    own = lax.dynamic_index_in_dim(blocks, me, 0, keepdims=False).astype(jnp.float32)
    if count == 1:
        return own.astype(parts.dtype)

    def run(step_block, pairs_of):
        received = None
        for step in range(1, count):
            block = lax.dynamic_index_in_dim(
                blocks, jnp.clip(step_block(step), 0, count - 1), 0, keepdims=False
            )
            if received is not None:
                block = (received.astype(jnp.float32) + block.astype(jnp.float32)).astype(
                    parts.dtype
                )
            received = lax.ppermute(block, axis, pairs_of(step))
        return received.astype(jnp.float32)

    rightward = run(
        lambda step: me + count - step,
        lambda step: [(src, src + 1) for src in range(step) if src + 1 < count],
    )
    leftward = run(
        lambda step: me - count + step,
        lambda step: [(src, src - 1) for src in range(count - step, count) if src >= 1],
    )
    return (own + rightward + leftward).astype(parts.dtype)


def exchange_reduce(rows, weight, axis):
    count = lax.axis_size(axis)
    me = lax.axis_index(axis)
    span = rows.shape[0] // count
    total = None
    for shift in list(range(1, count)) + [0]:
        target = lax.rem(me + shift, count)
        block_rows = lax.dynamic_slice_in_dim(rows, target * span, span, 0)
        part = jnp.dot(block_rows, weight, preferred_element_type=jnp.float32).astype(jnp.bfloat16)
        if shift:
            part = lax.ppermute(part, axis, [(src, (src + shift) % count) for src in range(count)])
        part = part.astype(jnp.float32)
        total = part if total is None else total + part
    return total.astype(jnp.bfloat16)


def shards(
    tokens,
    norm_gain,
    router_weight,
    kv_weight,
    query_weight,
    out_weight,
    expert_ids,
    lengths,
    kv_cache,
):
    normed = normalize(tokens, norm_gain)
    tok_count = normed.shape[0]
    experts = query_weight.shape[0]
    head_dim = kv_cache.shape[3] // 2
    local_heads = query_weight.shape[2] // head_dim
    cache_len = kv_cache.shape[2]
    block_len = min(512, cache_len // 4)
    gate_values = gate_pair(normed, router_weight, expert_ids)
    query_full = lax.all_gather(query_weight, "req", axis=1, tiled=True)
    query_full, kv_weight, out_weight = lax.optimization_barrier(
        (query_full, kv_weight, out_weight)
    )
    kv_full = lax.all_gather(kv_weight, "req", axis=0, tiled=True)
    out_full = lax.all_gather(out_weight, "req", axis=2, tiled=True)
    projected = jnp.dot(normed, kv_full, preferred_element_type=jnp.float32)
    query_all = jnp.einsum(
        "tc,ecn->ten", normed, query_full, preferred_element_type=jnp.float32
    )
    req_index = lax.axis_index("req")
    own_length = pick_length(lengths, req_index)
    positions = (own_length + jnp.arange(tok_count)).astype(jnp.float32)
    projected = projected.reshape(tok_count, local_heads, 2, head_dim)
    new_keys = rotate(jnp.transpose(projected[:, :, 0], (1, 0, 2)), positions)
    new_values = jnp.transpose(projected[:, :, 1], (1, 0, 2))
    fresh_kv = jnp.concatenate([new_keys, new_values], axis=-1).astype(jnp.bfloat16)
    one_hot = jnp.arange(experts)[None, None, :] == expert_ids[:, :, None]
    query_sel = jnp.sum(jnp.where(one_hot[..., None], query_all[:, None], 0.0), axis=2)
    queries = jnp.transpose(query_sel.reshape(tok_count * 2, local_heads, head_dim), (1, 0, 2))
    queries = rotate(queries, jnp.repeat(positions, 2)).astype(jnp.bfloat16)
    own_cache = kv_cache[0]
    query_rows = tok_count * 2
    empty_state = (
        jnp.full((local_heads, query_rows), NEG_LARGE, jnp.float32),
        jnp.zeros((local_heads, query_rows), jnp.float32),
        jnp.zeros((local_heads, query_rows, head_dim), jnp.float32),
    )
    carry_state = cache_pass(
        queries,
        own_cache,
        0,
        own_length,
        0,
        (own_length + block_len - 1) // block_len,
        0,
        block_len,
        empty_state,
    )
    row_ids = jnp.arange(query_rows) // 2
    causal = row_ids[:, None] >= jnp.arange(tok_count)[None, :]
    carry_state = absorb(
        carry_state, queries, fresh_kv[..., :head_dim], fresh_kv[..., head_dim:], causal
    )
    heads_out = carry_state[2] / carry_state[1][..., None]
    heads_out = jnp.transpose(heads_out, (1, 0, 2)).reshape(tok_count, 2, local_heads * head_dim)
    weighted = (gate_values[:, :, None] * heads_out).astype(jnp.bfloat16)
    mixture = jnp.sum(jnp.where(one_hot[..., None], weighted[:, :, None, :], 0), axis=1)
    mixture_flat = mixture.reshape(tok_count, experts * local_heads * head_dim)
    flat_piece = out_full.reshape(experts * local_heads * head_dim, out_full.shape[2])
    result = exchange_reduce(mixture_flat, flat_piece, "head")
    return (result, fresh_kv[None])


def solution(mesh):
    placed = (
        P("req", None),
        P(),
        P(),
        P("req", "head"),
        P(None, "req", "head"),
        P(None, "head", "req"),
        P("req", None),
        P(),
        P("req", "head", None, None),
    )
    return jax.shard_map(
        shards,
        mesh=mesh,
        in_specs=placed,
        out_specs=(P(("req", "head"), None), P("req", "head", None, None)),
        check_vma=False,
    )
```

```python
import functools
import math

import jax
import jax.numpy as jnp
from jax import lax
from jax.experimental import pallas as pl
from jax.experimental.pallas import tpu as pltpu
from jax.sharding import PartitionSpec as P

NEG_LARGE = -1e30
EPSILON = 1e-06


def normalize(tokens, norm_gain):
    widened = tokens.astype(jnp.float32)
    factor = lax.rsqrt(jnp.mean(widened * widened, axis=-1, keepdims=True) + EPSILON)
    return (widened * factor * norm_gain).astype(jnp.bfloat16)


def gate_pair(normed, router_weight, expert_ids):
    logits = jnp.dot(normed.astype(jnp.float32), router_weight, precision=lax.Precision.HIGHEST)
    one_hot = jnp.arange(router_weight.shape[1])[None, None, :] == expert_ids[:, :, None]
    chosen = jnp.sum(jnp.where(one_hot, logits[:, None, :], 0.0), axis=-1)
    logit_gap = chosen[:, 1] - chosen[:, 0]
    return jnp.stack([1.0 / (1.0 + jnp.exp(logit_gap)), 1.0 / (1.0 + jnp.exp(-logit_gap))], axis=1)


def rotate(vectors, positions):
    half_dim = vectors.shape[-1] // 2
    inv_freq = jnp.exp(-math.log(10000.0) * jnp.arange(half_dim, dtype=jnp.float32) / half_dim)
    angles = positions[:, None] * inv_freq[None, :]
    cosine_table = jnp.cos(angles)
    sine_table = jnp.sin(angles)
    front_half = vectors[..., :half_dim]
    back_half = vectors[..., half_dim:]
    return jnp.concatenate(
        [
            front_half * cosine_table - back_half * sine_table,
            back_half * cosine_table + front_half * sine_table,
        ],
        axis=-1,
    )


def pick_length(lengths, wanted):
    return jnp.sum(jnp.where(jnp.arange(lengths.shape[0]) == wanted, lengths, 0))


def absorb(carry_state, queries, key_rows, value_rows, allowed):
    row_peak, row_total, row_accum = carry_state
    scale_factor = queries.shape[-1] ** (-0.5)
    scores = (
        jnp.einsum("hqd,hkd->hqk", queries, key_rows, preferred_element_type=jnp.float32)
        * scale_factor
    )
    scores = jnp.where(allowed[None], scores, NEG_LARGE)
    new_peak = jnp.maximum(row_peak, jnp.max(scores, axis=-1))
    weights = jnp.where(allowed[None], jnp.exp(scores - new_peak[..., None]), 0.0)
    shrink = jnp.exp(row_peak - new_peak)
    row_total = row_total * shrink + jnp.sum(weights, axis=-1)
    row_accum = row_accum * shrink[..., None] + jnp.einsum(
        "hqk,hkd->hqd", weights.astype(jnp.bfloat16), value_rows, preferred_element_type=jnp.float32
    )
    return (new_peak, row_total, row_accum)


def cache_pass(
    queries, source, lowest, highest, first_block, last_block, anchor, block_len, carry_state
):
    head_dim = source.shape[2] // 2

    def block_step(block_id, running):
        block_rows = lax.dynamic_slice_in_dim(source, block_id * block_len, block_len, 1)
        key_index = anchor + block_id * block_len + jnp.arange(block_len)
        allowed = ((key_index >= lowest) & (key_index < highest))[None, :]
        return absorb(
            running, queries, block_rows[..., :head_dim], block_rows[..., head_dim:], allowed
        )

    return lax.fori_loop(
        jnp.asarray(first_block, jnp.int32),
        jnp.asarray(last_block, jnp.int32),
        block_step,
        carry_state,
    )


def chain_reduce(parts, axis):
    count = lax.axis_size(axis)
    me = lax.axis_index(axis)
    blocks = parts.reshape(count, parts.shape[0] // count, parts.shape[1])
    own = lax.dynamic_index_in_dim(blocks, me, 0, keepdims=False).astype(jnp.float32)
    if count == 1:
        return own.astype(parts.dtype)

    def run(step_block, pairs_of):
        received = None
        for step in range(1, count):
            block = lax.dynamic_index_in_dim(
                blocks, jnp.clip(step_block(step), 0, count - 1), 0, keepdims=False
            )
            if received is not None:
                block = (received.astype(jnp.float32) + block.astype(jnp.float32)).astype(
                    parts.dtype
                )
            received = lax.ppermute(block, axis, pairs_of(step))
        return received.astype(jnp.float32)

    rightward = run(
        lambda step: me + count - step,
        lambda step: [(src, src + 1) for src in range(step) if src + 1 < count],
    )
    leftward = run(
        lambda step: me - count + step,
        lambda step: [(src, src - 1) for src in range(count - step, count) if src >= 1],
    )
    return (own + rightward + leftward).astype(parts.dtype)


def exchange_reduce(rows, weight, axis):
    count = lax.axis_size(axis)
    me = lax.axis_index(axis)
    span = rows.shape[0] // count
    total = None
    for shift in list(range(1, count)) + [0]:
        target = lax.rem(me + shift, count)
        block_rows = lax.dynamic_slice_in_dim(rows, target * span, span, 0)
        part = jnp.dot(block_rows, weight, preferred_element_type=jnp.float32).astype(jnp.bfloat16)
        if shift:
            part = lax.ppermute(part, axis, [(src, (src + shift) % count) for src in range(count)])
        part = part.astype(jnp.float32)
        total = part if total is None else total + part
    return total.astype(jnp.bfloat16)


def attention_kernel(
    length_ref, q_ref, cache_ref, fresh_ref, out_ref, peak_ref, total_ref, accum_ref, *, cache_blocks
):
    q_block = pl.program_id(1)
    kv_block = pl.program_id(2)
    rows, head_dim = q_ref.shape[1], q_ref.shape[2]
    span = cache_ref.shape[1]
    length = length_ref[0]

    @pl.when(kv_block == 0)
    def _():
        peak_ref[...] = jnp.full(peak_ref.shape, NEG_LARGE, jnp.float32)
        total_ref[...] = jnp.zeros(total_ref.shape, jnp.float32)
        accum_ref[...] = jnp.zeros(accum_ref.shape, jnp.float32)

    def absorb_block(block, allowed):
        queries = q_ref[0]
        scores = lax.dot_general(
            queries,
            block[:, :head_dim],
            (((1,), (1,)), ((), ())),
            preferred_element_type=jnp.float32,
        ) * (head_dim ** (-0.5))
        scores = jnp.where(allowed, scores, NEG_LARGE)
        old_peak = peak_ref[...]
        new_peak = jnp.maximum(old_peak, jnp.max(scores, axis=-1, keepdims=True))
        weights = jnp.where(allowed, jnp.exp(scores - new_peak), 0.0)
        shrink = jnp.exp(old_peak - new_peak)
        total_ref[...] = total_ref[...] * shrink + jnp.sum(weights, axis=-1, keepdims=True)
        accum_ref[...] = accum_ref[...] * shrink + jnp.dot(
            weights.astype(jnp.bfloat16), block[:, head_dim:], preferred_element_type=jnp.float32
        )
        peak_ref[...] = new_peak

    @pl.when((kv_block < cache_blocks) & (kv_block * span < length))
    def _():
        key_index = kv_block * span + lax.broadcasted_iota(jnp.int32, (1, span), 1)
        absorb_block(cache_ref[0], key_index < length)

    @pl.when(kv_block == cache_blocks)
    def _():
        row_token = (q_block * rows + lax.broadcasted_iota(jnp.int32, (rows, 1), 0)) // 2
        key_index = lax.broadcasted_iota(jnp.int32, (1, span), 1)
        absorb_block(fresh_ref[0], key_index <= row_token)
        out_ref[0] = accum_ref[...] / total_ref[...]


def attend(queries, cache, fresh, length):
    heads, query_rows, head_dim = queries.shape
    span = fresh.shape[1]
    cache_blocks = cache.shape[1] // span
    rows = min(query_rows, 512)

    def cache_map(h, i, j, length_ref):
        last = jnp.maximum((length_ref[0] + span - 1) // span - 1, 0)
        return (h, jnp.minimum(j, last), 0)

    grid_spec = pltpu.PrefetchScalarGridSpec(
        num_scalar_prefetch=1,
        grid=(heads, query_rows // rows, cache_blocks + 1),
        in_specs=[
            pl.BlockSpec((1, rows, head_dim), lambda h, i, j, length_ref: (h, i, 0)),
            pl.BlockSpec((1, span, 2 * head_dim), cache_map),
            pl.BlockSpec((1, span, 2 * head_dim), lambda h, i, j, length_ref: (h, 0, 0)),
        ],
        out_specs=pl.BlockSpec((1, rows, head_dim), lambda h, i, j, length_ref: (h, i, 0)),
        scratch_shapes=[
            pltpu.VMEM((rows, 1), jnp.float32),
            pltpu.VMEM((rows, 1), jnp.float32),
            pltpu.VMEM((rows, head_dim), jnp.float32),
        ],
    )
    keys_seen = 4 * heads * query_rows * (cache.shape[1] + span) * head_dim
    return pl.pallas_call(
        functools.partial(attention_kernel, cache_blocks=cache_blocks),
        out_shape=jax.ShapeDtypeStruct((heads, query_rows, head_dim), jnp.float32),
        grid_spec=grid_spec,
        compiler_params=pltpu.CompilerParams(
            dimension_semantics=("arbitrary", "arbitrary", "arbitrary")
        ),
        cost_estimate=pl.CostEstimate(
            flops=keys_seen,
            transcendentals=heads * query_rows * (cache.shape[1] + span),
            bytes_accessed=2 * (cache.size + fresh.size + queries.size) + 4 * queries.size,
        ),
    )(jnp.reshape(length, (1,)).astype(jnp.int32), queries, cache, fresh)


def shards(
    tokens,
    norm_gain,
    router_weight,
    kv_weight,
    query_weight,
    out_weight,
    expert_ids,
    lengths,
    kv_cache,
):
    normed = normalize(tokens, norm_gain)
    tok_count = normed.shape[0]
    experts = query_weight.shape[0]
    head_dim = kv_cache.shape[3] // 2
    local_heads = query_weight.shape[2] // head_dim
    cache_len = kv_cache.shape[2]
    block_len = min(512, cache_len // 4)
    gate_values = gate_pair(normed, router_weight, expert_ids)
    query_full = lax.all_gather(query_weight, "req", axis=1, tiled=True)
    query_full, kv_weight, out_weight = lax.optimization_barrier(
        (query_full, kv_weight, out_weight)
    )
    kv_full = lax.all_gather(kv_weight, "req", axis=0, tiled=True)
    out_full = lax.all_gather(out_weight, "req", axis=2, tiled=True)
    projected = jnp.dot(normed, kv_full, preferred_element_type=jnp.float32)
    query_all = jnp.einsum(
        "tc,ecn->ten", normed, query_full, preferred_element_type=jnp.float32
    )
    req_index = lax.axis_index("req")
    own_length = pick_length(lengths, req_index)
    positions = (own_length + jnp.arange(tok_count)).astype(jnp.float32)
    projected = projected.reshape(tok_count, local_heads, 2, head_dim)
    new_keys = rotate(jnp.transpose(projected[:, :, 0], (1, 0, 2)), positions)
    new_values = jnp.transpose(projected[:, :, 1], (1, 0, 2))
    fresh_kv = jnp.concatenate([new_keys, new_values], axis=-1).astype(jnp.bfloat16)
    one_hot = jnp.arange(experts)[None, None, :] == expert_ids[:, :, None]
    query_sel = jnp.sum(jnp.where(one_hot[..., None], query_all[:, None], 0.0), axis=2)
    queries = jnp.transpose(query_sel.reshape(tok_count * 2, local_heads, head_dim), (1, 0, 2))
    queries = rotate(queries, jnp.repeat(positions, 2)).astype(jnp.bfloat16)
    heads_out = attend(queries, kv_cache[0], fresh_kv, own_length)
    heads_out = jnp.transpose(heads_out, (1, 0, 2)).reshape(tok_count, 2, local_heads * head_dim)
    weighted = (gate_values[:, :, None] * heads_out).astype(jnp.bfloat16)
    mixture = jnp.sum(jnp.where(one_hot[..., None], weighted[:, :, None, :], 0), axis=1)
    mixture_flat = mixture.reshape(tok_count, experts * local_heads * head_dim)
    flat_piece = out_full.reshape(experts * local_heads * head_dim, out_full.shape[2])
    result = exchange_reduce(mixture_flat, flat_piece, "head")
    return (result, fresh_kv[None])


def solution(mesh):
    placed = (
        P("req", None),
        P(),
        P(),
        P("req", "head"),
        P(None, "req", "head"),
        P(None, "head", "req"),
        P("req", None),
        P(),
        P("req", "head", None, None),
    )
    return jax.shard_map(
        shards,
        mesh=mesh,
        in_specs=placed,
        out_specs=(P(("req", "head"), None), P("req", "head", None, None)),
        check_vma=False,
    )
```

```python
import functools
import math

import jax
import jax.numpy as jnp
from jax import lax
from jax.experimental import pallas as pl
from jax.experimental.pallas import tpu as pltpu
from jax.sharding import PartitionSpec as P

NEG_LARGE = -1e30
EPSILON = 1e-06


def normalize(tokens, norm_gain):
    widened = tokens.astype(jnp.float32)
    factor = lax.rsqrt(jnp.mean(widened * widened, axis=-1, keepdims=True) + EPSILON)
    return (widened * factor * norm_gain).astype(jnp.bfloat16)


def gate_pair(normed, router_weight, expert_ids):
    logits = jnp.dot(normed.astype(jnp.float32), router_weight, precision=lax.Precision.HIGHEST)
    one_hot = jnp.arange(router_weight.shape[1])[None, None, :] == expert_ids[:, :, None]
    chosen = jnp.sum(jnp.where(one_hot, logits[:, None, :], 0.0), axis=-1)
    logit_gap = chosen[:, 1] - chosen[:, 0]
    return jnp.stack([1.0 / (1.0 + jnp.exp(logit_gap)), 1.0 / (1.0 + jnp.exp(-logit_gap))], axis=1)


def rotate(vectors, positions):
    half_dim = vectors.shape[-1] // 2
    inv_freq = jnp.exp(-math.log(10000.0) * jnp.arange(half_dim, dtype=jnp.float32) / half_dim)
    angles = positions[:, None] * inv_freq[None, :]
    cosine_table = jnp.cos(angles)
    sine_table = jnp.sin(angles)
    front_half = vectors[..., :half_dim]
    back_half = vectors[..., half_dim:]
    return jnp.concatenate(
        [
            front_half * cosine_table - back_half * sine_table,
            back_half * cosine_table + front_half * sine_table,
        ],
        axis=-1,
    )


def pick_length(lengths, wanted):
    return jnp.sum(jnp.where(jnp.arange(lengths.shape[0]) == wanted, lengths, 0))


def absorb(carry_state, queries, key_rows, value_rows, allowed):
    row_peak, row_total, row_accum = carry_state
    scale_factor = queries.shape[-1] ** (-0.5)
    scores = (
        jnp.einsum("hqd,hkd->hqk", queries, key_rows, preferred_element_type=jnp.float32)
        * scale_factor
    )
    scores = jnp.where(allowed[None], scores, NEG_LARGE)
    new_peak = jnp.maximum(row_peak, jnp.max(scores, axis=-1))
    weights = jnp.where(allowed[None], jnp.exp(scores - new_peak[..., None]), 0.0)
    shrink = jnp.exp(row_peak - new_peak)
    row_total = row_total * shrink + jnp.sum(weights, axis=-1)
    row_accum = row_accum * shrink[..., None] + jnp.einsum(
        "hqk,hkd->hqd", weights.astype(jnp.bfloat16), value_rows, preferred_element_type=jnp.float32
    )
    return (new_peak, row_total, row_accum)


def cache_pass(
    queries, source, lowest, highest, first_block, last_block, anchor, block_len, carry_state
):
    head_dim = source.shape[2] // 2

    def block_step(block_id, running):
        block_rows = lax.dynamic_slice_in_dim(source, block_id * block_len, block_len, 1)
        key_index = anchor + block_id * block_len + jnp.arange(block_len)
        allowed = ((key_index >= lowest) & (key_index < highest))[None, :]
        return absorb(
            running, queries, block_rows[..., :head_dim], block_rows[..., head_dim:], allowed
        )

    return lax.fori_loop(
        jnp.asarray(first_block, jnp.int32),
        jnp.asarray(last_block, jnp.int32),
        block_step,
        carry_state,
    )


def chain_reduce(parts, axis):
    count = lax.axis_size(axis)
    me = lax.axis_index(axis)
    blocks = parts.reshape(count, parts.shape[0] // count, parts.shape[1])
    own = lax.dynamic_index_in_dim(blocks, me, 0, keepdims=False).astype(jnp.float32)
    if count == 1:
        return own.astype(parts.dtype)

    def run(step_block, pairs_of):
        received = None
        for step in range(1, count):
            block = lax.dynamic_index_in_dim(
                blocks, jnp.clip(step_block(step), 0, count - 1), 0, keepdims=False
            )
            if received is not None:
                block = (received.astype(jnp.float32) + block.astype(jnp.float32)).astype(
                    parts.dtype
                )
            received = lax.ppermute(block, axis, pairs_of(step))
        return received.astype(jnp.float32)

    rightward = run(
        lambda step: me + count - step,
        lambda step: [(src, src + 1) for src in range(step) if src + 1 < count],
    )
    leftward = run(
        lambda step: me - count + step,
        lambda step: [(src, src - 1) for src in range(count - step, count) if src >= 1],
    )
    return (own + rightward + leftward).astype(parts.dtype)


def exchange_reduce(rows, weight, axis):
    count = lax.axis_size(axis)
    me = lax.axis_index(axis)
    span = rows.shape[0] // count
    total = None
    for shift in list(range(1, count)) + [0]:
        target = lax.rem(me + shift, count)
        block_rows = lax.dynamic_slice_in_dim(rows, target * span, span, 0)
        part = jnp.dot(block_rows, weight, preferred_element_type=jnp.float32).astype(jnp.bfloat16)
        if shift:
            part = lax.ppermute(part, axis, [(src, (src + shift) % count) for src in range(count)])
        part = part.astype(jnp.float32)
        total = part if total is None else total + part
    return total.astype(jnp.bfloat16)


def attention_kernel(
    length_ref, q_ref, cache_ref, fresh_ref, out_ref, peak_ref, total_ref, accum_ref, *, cache_blocks
):
    q_block = pl.program_id(1)
    kv_block = pl.program_id(2)
    rows, head_dim = q_ref.shape
    span = cache_ref.shape[1]
    length = length_ref[0]

    @pl.when(kv_block == 0)
    def _():
        peak_ref[...] = jnp.full(peak_ref.shape, NEG_LARGE, jnp.float32)
        total_ref[...] = jnp.zeros(total_ref.shape, jnp.float32)
        accum_ref[...] = jnp.zeros(accum_ref.shape, jnp.float32)

    def absorb_block(block, allowed):
        queries = q_ref[...]
        scores = lax.dot_general(
            queries,
            block[:, :head_dim],
            (((1,), (1,)), ((), ())),
            preferred_element_type=jnp.float32,
        ) * (head_dim ** (-0.5))
        scores = jnp.where(allowed, scores, NEG_LARGE)
        old_peak = peak_ref[...]
        new_peak = jnp.maximum(old_peak, jnp.max(scores, axis=-1, keepdims=True))
        weights = jnp.where(allowed, jnp.exp(scores - new_peak), 0.0)
        shrink = jnp.exp(old_peak - new_peak)
        total_ref[...] = total_ref[...] * shrink + jnp.sum(weights, axis=-1, keepdims=True)
        accum_ref[...] = accum_ref[...] * shrink + jnp.dot(
            weights.astype(jnp.bfloat16), block[:, head_dim:], preferred_element_type=jnp.float32
        )
        peak_ref[...] = new_peak

    @pl.when((kv_block < cache_blocks) & (kv_block * span < length))
    def _():
        key_index = kv_block * span + lax.broadcasted_iota(jnp.int32, (1, span), 1)
        absorb_block(cache_ref[0], key_index < length)

    @pl.when(kv_block == cache_blocks)
    def _():
        row_token = (q_block * rows + lax.broadcasted_iota(jnp.int32, (rows, 1), 0)) % span
        key_index = lax.broadcasted_iota(jnp.int32, (1, span), 1)
        absorb_block(fresh_ref[0], key_index <= row_token)
        out_ref[...] = accum_ref[...] / total_ref[...]


def attend(queries, cache, fresh, length):
    heads, span, head_dim = fresh.shape[0], fresh.shape[1], fresh.shape[2] // 2
    query_rows = queries.shape[0]
    cache_blocks = cache.shape[1] // span
    rows = min(query_rows, 512)

    def cache_map(h, i, j, length_ref):
        last = jnp.maximum((length_ref[0] + span - 1) // span - 1, 0)
        return (h, jnp.minimum(j, last), 0)

    grid_spec = pltpu.PrefetchScalarGridSpec(
        num_scalar_prefetch=1,
        grid=(heads, query_rows // rows, cache_blocks + 1),
        in_specs=[
            pl.BlockSpec((rows, head_dim), lambda h, i, j, length_ref: (i, h)),
            pl.BlockSpec((1, span, 2 * head_dim), cache_map),
            pl.BlockSpec((1, span, 2 * head_dim), lambda h, i, j, length_ref: (h, 0, 0)),
        ],
        out_specs=pl.BlockSpec((rows, head_dim), lambda h, i, j, length_ref: (i, h)),
        scratch_shapes=[
            pltpu.VMEM((rows, 1), jnp.float32),
            pltpu.VMEM((rows, 1), jnp.float32),
            pltpu.VMEM((rows, head_dim), jnp.float32),
        ],
    )
    keys_seen = 4 * heads * query_rows * (cache.shape[1] + span) * head_dim
    return pl.pallas_call(
        functools.partial(attention_kernel, cache_blocks=cache_blocks),
        out_shape=jax.ShapeDtypeStruct(queries.shape, jnp.float32),
        grid_spec=grid_spec,
        compiler_params=pltpu.CompilerParams(
            dimension_semantics=("arbitrary", "arbitrary", "arbitrary")
        ),
        cost_estimate=pl.CostEstimate(
            flops=keys_seen,
            transcendentals=heads * query_rows * (cache.shape[1] + span),
            bytes_accessed=2 * (cache.size + fresh.size + queries.size) + 4 * queries.size,
        ),
    )(jnp.reshape(length, (1,)).astype(jnp.int32), queries, cache, fresh)


def shards(
    tokens,
    norm_gain,
    router_weight,
    kv_weight,
    query_weight,
    out_weight,
    expert_ids,
    lengths,
    kv_cache,
):
    normed = normalize(tokens, norm_gain)
    tok_count = normed.shape[0]
    experts = query_weight.shape[0]
    head_dim = kv_cache.shape[3] // 2
    local_heads = query_weight.shape[2] // head_dim
    cache_len = kv_cache.shape[2]
    block_len = min(512, cache_len // 4)
    gate_values = gate_pair(normed, router_weight, expert_ids)
    query_full = lax.all_gather(query_weight, "req", axis=1, tiled=True)
    query_full, kv_weight, out_weight = lax.optimization_barrier(
        (query_full, kv_weight, out_weight)
    )
    kv_full = lax.all_gather(kv_weight, "req", axis=0, tiled=True)
    out_full = lax.all_gather(out_weight, "req", axis=2, tiled=True)
    projected = jnp.dot(normed, kv_full, preferred_element_type=jnp.float32)
    query_all = jnp.einsum(
        "tc,ecn->etn", normed, query_full, preferred_element_type=jnp.float32
    )
    req_index = lax.axis_index("req")
    own_length = pick_length(lengths, req_index)
    positions = (own_length + jnp.arange(tok_count)).astype(jnp.float32)
    projected = projected.reshape(tok_count, local_heads, 2, head_dim)
    new_keys = rotate(jnp.transpose(projected[:, :, 0], (1, 0, 2)), positions)
    new_values = jnp.transpose(projected[:, :, 1], (1, 0, 2))
    fresh_kv = jnp.concatenate([new_keys, new_values], axis=-1).astype(jnp.bfloat16)
    one_hot = jnp.arange(experts)[None, None, :] == expert_ids[:, :, None]
    choice_hot = jnp.transpose(one_hot, (1, 2, 0))
    query_sel = jnp.sum(jnp.where(choice_hot[..., None], query_all[None], 0.0), axis=1)
    query_sel = query_sel.reshape(2, tok_count, local_heads, head_dim)
    queries = rotate(query_sel, positions[:, None]).astype(jnp.bfloat16)
    queries = queries.reshape(2 * tok_count, local_heads * head_dim)
    heads_out = attend(queries, kv_cache[0], fresh_kv, own_length)
    heads_out = heads_out.reshape(2, tok_count, local_heads * head_dim)
    weighted = (jnp.transpose(gate_values)[:, :, None] * heads_out).astype(jnp.bfloat16)
    token_hot = jnp.transpose(one_hot, (1, 0, 2))
    mixture = jnp.sum(jnp.where(token_hot[..., None], weighted[:, :, None, :], 0), axis=0)
    mixture_flat = mixture.reshape(tok_count, experts * local_heads * head_dim)
    flat_piece = out_full.reshape(experts * local_heads * head_dim, out_full.shape[2])
    result = exchange_reduce(mixture_flat, flat_piece, "head")
    return (result, fresh_kv[None])


def solution(mesh):
    placed = (
        P("req", None),
        P(),
        P(),
        P("req", "head"),
        P(None, "req", "head"),
        P(None, "head", "req"),
        P("req", None),
        P(),
        P("req", "head", None, None),
    )
    return jax.shard_map(
        shards,
        mesh=mesh,
        in_specs=placed,
        out_specs=(P(("req", "head"), None), P("req", "head", None, None)),
        check_vma=False,
    )
```

```python
import functools
import math

import jax
import jax.numpy as jnp
from jax import lax
from jax.experimental import pallas as pl
from jax.experimental.pallas import tpu as pltpu
from jax.sharding import PartitionSpec as P

NEG_LARGE = -1e30
EPSILON = 1e-06


def normalize(tokens, norm_gain):
    widened = tokens.astype(jnp.float32)
    factor = lax.rsqrt(jnp.mean(widened * widened, axis=-1, keepdims=True) + EPSILON)
    return (widened * factor * norm_gain).astype(jnp.bfloat16)


def gate_pair(normed, router_weight, expert_ids):
    logits = jnp.dot(normed.astype(jnp.float32), router_weight, precision=lax.Precision.HIGHEST)
    one_hot = jnp.arange(router_weight.shape[1])[None, None, :] == expert_ids[:, :, None]
    chosen = jnp.sum(jnp.where(one_hot, logits[:, None, :], 0.0), axis=-1)
    logit_gap = chosen[:, 1] - chosen[:, 0]
    return jnp.stack([1.0 / (1.0 + jnp.exp(logit_gap)), 1.0 / (1.0 + jnp.exp(-logit_gap))], axis=1)


def rotate(vectors, positions):
    half_dim = vectors.shape[-1] // 2
    inv_freq = jnp.exp(-math.log(10000.0) * jnp.arange(half_dim, dtype=jnp.float32) / half_dim)
    angles = positions[:, None] * inv_freq[None, :]
    cosine_table = jnp.cos(angles)
    sine_table = jnp.sin(angles)
    front_half = vectors[..., :half_dim]
    back_half = vectors[..., half_dim:]
    return jnp.concatenate(
        [
            front_half * cosine_table - back_half * sine_table,
            back_half * cosine_table + front_half * sine_table,
        ],
        axis=-1,
    )


def pick_length(lengths, wanted):
    return jnp.sum(jnp.where(jnp.arange(lengths.shape[0]) == wanted, lengths, 0))


def absorb(carry_state, queries, key_rows, value_rows, allowed):
    row_peak, row_total, row_accum = carry_state
    scale_factor = queries.shape[-1] ** (-0.5)
    scores = (
        jnp.einsum("hqd,hkd->hqk", queries, key_rows, preferred_element_type=jnp.float32)
        * scale_factor
    )
    scores = jnp.where(allowed[None], scores, NEG_LARGE)
    new_peak = jnp.maximum(row_peak, jnp.max(scores, axis=-1))
    weights = jnp.where(allowed[None], jnp.exp(scores - new_peak[..., None]), 0.0)
    shrink = jnp.exp(row_peak - new_peak)
    row_total = row_total * shrink + jnp.sum(weights, axis=-1)
    row_accum = row_accum * shrink[..., None] + jnp.einsum(
        "hqk,hkd->hqd", weights.astype(jnp.bfloat16), value_rows, preferred_element_type=jnp.float32
    )
    return (new_peak, row_total, row_accum)


def cache_pass(
    queries, source, lowest, highest, first_block, last_block, anchor, block_len, carry_state
):
    head_dim = source.shape[2] // 2

    def block_step(block_id, running):
        block_rows = lax.dynamic_slice_in_dim(source, block_id * block_len, block_len, 1)
        key_index = anchor + block_id * block_len + jnp.arange(block_len)
        allowed = ((key_index >= lowest) & (key_index < highest))[None, :]
        return absorb(
            running, queries, block_rows[..., :head_dim], block_rows[..., head_dim:], allowed
        )

    return lax.fori_loop(
        jnp.asarray(first_block, jnp.int32),
        jnp.asarray(last_block, jnp.int32),
        block_step,
        carry_state,
    )


def chain_reduce(parts, axis):
    count = lax.axis_size(axis)
    me = lax.axis_index(axis)
    blocks = parts.reshape(count, parts.shape[0] // count, parts.shape[1])
    own = lax.dynamic_index_in_dim(blocks, me, 0, keepdims=False).astype(jnp.float32)
    if count == 1:
        return own.astype(parts.dtype)

    def run(step_block, pairs_of):
        received = None
        for step in range(1, count):
            block = lax.dynamic_index_in_dim(
                blocks, jnp.clip(step_block(step), 0, count - 1), 0, keepdims=False
            )
            if received is not None:
                block = (received.astype(jnp.float32) + block.astype(jnp.float32)).astype(
                    parts.dtype
                )
            received = lax.ppermute(block, axis, pairs_of(step))
        return received.astype(jnp.float32)

    rightward = run(
        lambda step: me + count - step,
        lambda step: [(src, src + 1) for src in range(step) if src + 1 < count],
    )
    leftward = run(
        lambda step: me - count + step,
        lambda step: [(src, src - 1) for src in range(count - step, count) if src >= 1],
    )
    return (own + rightward + leftward).astype(parts.dtype)


def exchange_parts(rows, weight, axis):
    count = lax.axis_size(axis)
    me = lax.axis_index(axis)
    span = rows.shape[0] // count
    parts = []
    for shift in list(range(1, count)) + [0]:
        target = lax.rem(me + shift, count)
        block_rows = lax.dynamic_slice_in_dim(rows, target * span, span, 0)
        parts.append(
            jnp.dot(block_rows, weight, preferred_element_type=jnp.float32).astype(jnp.bfloat16)
        )
    return parts


def exchange_finish(parts, axis):
    count = lax.axis_size(axis)
    total = parts[-1].astype(jnp.float32)
    for shift, part in zip(range(1, count), parts):
        moved = lax.ppermute(part, axis, [(src, (src + shift) % count) for src in range(count)])
        total = total + moved.astype(jnp.float32)
    return total.astype(jnp.bfloat16)

def attention_kernel(
    length_ref, q_ref, cache_ref, fresh_ref, out_ref, peak_ref, total_ref, accum_ref, *, cache_blocks
):
    q_block = pl.program_id(1)
    kv_block = pl.program_id(2)
    rows, head_dim = q_ref.shape
    span = cache_ref.shape[1]
    length = length_ref[0]

    @pl.when(kv_block == 0)
    def _():
        peak_ref[...] = jnp.full(peak_ref.shape, NEG_LARGE, jnp.float32)
        total_ref[...] = jnp.zeros(total_ref.shape, jnp.float32)
        accum_ref[...] = jnp.zeros(accum_ref.shape, jnp.float32)

    def absorb_block(block, allowed):
        queries = q_ref[...]
        scores = lax.dot_general(
            queries,
            block[:, :head_dim],
            (((1,), (1,)), ((), ())),
            preferred_element_type=jnp.float32,
        ) * (head_dim ** (-0.5))
        scores = jnp.where(allowed, scores, NEG_LARGE)
        old_peak = peak_ref[...]
        new_peak = jnp.maximum(old_peak, jnp.max(scores, axis=-1, keepdims=True))
        weights = jnp.where(allowed, jnp.exp(scores - new_peak), 0.0)
        shrink = jnp.exp(old_peak - new_peak)
        total_ref[...] = total_ref[...] * shrink + jnp.sum(weights, axis=-1, keepdims=True)
        accum_ref[...] = accum_ref[...] * shrink + jnp.dot(
            weights.astype(jnp.bfloat16), block[:, head_dim:], preferred_element_type=jnp.float32
        )
        peak_ref[...] = new_peak

    @pl.when((kv_block < cache_blocks) & (kv_block * span < length))
    def _():
        key_index = kv_block * span + lax.broadcasted_iota(jnp.int32, (1, span), 1)
        absorb_block(cache_ref[0], key_index < length)

    @pl.when(kv_block == cache_blocks)
    def _():
        row_token = (q_block * rows + lax.broadcasted_iota(jnp.int32, (rows, 1), 0)) % span
        key_index = lax.broadcasted_iota(jnp.int32, (1, span), 1)
        absorb_block(fresh_ref[0], key_index <= row_token)
        out_ref[...] = accum_ref[...] / total_ref[...]


def attend(queries, cache, fresh, length):
    heads, span, head_dim = fresh.shape[0], fresh.shape[1], fresh.shape[2] // 2
    query_rows = queries.shape[0]
    cache_blocks = cache.shape[1] // span
    rows = min(query_rows, 512)

    def cache_map(h, i, j, length_ref):
        last = jnp.maximum((length_ref[0] + span - 1) // span - 1, 0)
        return (h, jnp.minimum(j, last), 0)

    grid_spec = pltpu.PrefetchScalarGridSpec(
        num_scalar_prefetch=1,
        grid=(heads, query_rows // rows, cache_blocks + 1),
        in_specs=[
            pl.BlockSpec((rows, head_dim), lambda h, i, j, length_ref: (i, h)),
            pl.BlockSpec((1, span, 2 * head_dim), cache_map),
            pl.BlockSpec((1, span, 2 * head_dim), lambda h, i, j, length_ref: (h, 0, 0)),
        ],
        out_specs=pl.BlockSpec((rows, head_dim), lambda h, i, j, length_ref: (i, h)),
        scratch_shapes=[
            pltpu.VMEM((rows, 1), jnp.float32),
            pltpu.VMEM((rows, 1), jnp.float32),
            pltpu.VMEM((rows, head_dim), jnp.float32),
        ],
    )
    keys_seen = 4 * heads * query_rows * (cache.shape[1] + span) * head_dim
    return pl.pallas_call(
        functools.partial(attention_kernel, cache_blocks=cache_blocks),
        out_shape=jax.ShapeDtypeStruct(queries.shape, jnp.float32),
        grid_spec=grid_spec,
        compiler_params=pltpu.CompilerParams(
            dimension_semantics=("arbitrary", "arbitrary", "arbitrary")
        ),
        cost_estimate=pl.CostEstimate(
            flops=keys_seen,
            transcendentals=heads * query_rows * (cache.shape[1] + span),
            bytes_accessed=2 * (cache.size + fresh.size + queries.size) + 4 * queries.size,
        ),
    )(jnp.reshape(length, (1,)).astype(jnp.int32), queries, cache, fresh)


def shards(
    tokens,
    norm_gain,
    router_weight,
    kv_weight,
    query_weight,
    out_weight,
    expert_ids,
    lengths,
    kv_cache,
):
    normed = normalize(tokens, norm_gain)
    tok_count = normed.shape[0]
    experts = query_weight.shape[0]
    head_dim = kv_cache.shape[3] // 2
    local_heads = query_weight.shape[2] // head_dim
    cache_len = kv_cache.shape[2]
    block_len = min(512, cache_len // 4)
    gate_values = gate_pair(normed, router_weight, expert_ids)
    query_full = lax.all_gather(query_weight, "req", axis=1, tiled=True)
    query_full, kv_weight, out_weight = lax.optimization_barrier(
        (query_full, kv_weight, out_weight)
    )
    kv_full = lax.all_gather(kv_weight, "req", axis=0, tiled=True)
    half = out_weight.shape[2] // 2
    out_halves = [
        lax.all_gather(piece, "req", axis=2, tiled=True)
        for piece in (out_weight[:, :, :half], out_weight[:, :, half:])
    ]
    projected = jnp.dot(normed, kv_full, preferred_element_type=jnp.float32)
    query_all = jnp.einsum(
        "tc,ecn->etn", normed, query_full, preferred_element_type=jnp.float32
    )
    req_index = lax.axis_index("req")
    own_length = pick_length(lengths, req_index)
    positions = (own_length + jnp.arange(tok_count)).astype(jnp.float32)
    projected = projected.reshape(tok_count, local_heads, 2, head_dim)
    new_keys = rotate(jnp.transpose(projected[:, :, 0], (1, 0, 2)), positions)
    new_values = jnp.transpose(projected[:, :, 1], (1, 0, 2))
    fresh_kv = jnp.concatenate([new_keys, new_values], axis=-1).astype(jnp.bfloat16)
    one_hot = jnp.arange(experts)[None, None, :] == expert_ids[:, :, None]
    choice_hot = jnp.transpose(one_hot, (1, 2, 0))
    query_sel = jnp.sum(jnp.where(choice_hot[..., None], query_all[None], 0.0), axis=1)
    query_sel = query_sel.reshape(2, tok_count, local_heads, head_dim)
    queries = rotate(query_sel, positions[:, None]).astype(jnp.bfloat16)
    queries = queries.reshape(2 * tok_count, local_heads * head_dim)
    heads_out = attend(queries, kv_cache[0], fresh_kv, own_length)
    heads_out = heads_out.reshape(2, tok_count, local_heads * head_dim)
    weighted = (jnp.transpose(gate_values)[:, :, None] * heads_out).astype(jnp.bfloat16)
    token_hot = jnp.transpose(one_hot, (1, 0, 2))
    mixture = jnp.sum(jnp.where(token_hot[..., None], weighted[:, :, None, :], 0), axis=0)
    mixture_flat = mixture.reshape(tok_count, experts * local_heads * head_dim)
    flat_halves = [
        piece.reshape(experts * local_heads * head_dim, piece.shape[2]) for piece in out_halves
    ]
    first_parts = exchange_parts(mixture_flat, flat_halves[0], "head")
    _, second_weight = lax.optimization_barrier((first_parts, flat_halves[1]))
    results = [
        exchange_finish(first_parts, "head"),
        exchange_finish(exchange_parts(mixture_flat, second_weight, "head"), "head"),
    ]
    column_blocks = out_halves[0].shape[2] // half
    result = jnp.stack(
        [part.reshape(part.shape[0], column_blocks, half) for part in results], axis=2
    ).reshape(results[0].shape[0], 2 * half * column_blocks)
    return (result, fresh_kv[None])


def solution(mesh):
    placed = (
        P("req", None),
        P(),
        P(),
        P("req", "head"),
        P(None, "req", "head"),
        P(None, "head", "req"),
        P("req", None),
        P(),
        P("req", "head", None, None),
    )
    return jax.shard_map(
        shards,
        mesh=mesh,
        in_specs=placed,
        out_specs=(P(("req", "head"), None), P("req", "head", None, None)),
        check_vma=False,
    )
```

```python
import functools
import math

import jax
import jax.numpy as jnp
from jax import lax
from jax.experimental import pallas as pl
from jax.experimental.pallas import tpu as pltpu
from jax.sharding import PartitionSpec as P

NEG_LARGE = -1e30
EPSILON = 1e-06


def normalize(tokens, norm_gain):
    widened = tokens.astype(jnp.float32)
    factor = lax.rsqrt(jnp.mean(widened * widened, axis=-1, keepdims=True) + EPSILON)
    return (widened * factor * norm_gain).astype(jnp.bfloat16)


def gate_pair(normed, router_weight, expert_ids):
    logits = jnp.dot(normed.astype(jnp.float32), router_weight, precision=lax.Precision.HIGHEST)
    one_hot = jnp.arange(router_weight.shape[1])[None, None, :] == expert_ids[:, :, None]
    chosen = jnp.sum(jnp.where(one_hot, logits[:, None, :], 0.0), axis=-1)
    logit_gap = chosen[:, 1] - chosen[:, 0]
    return jnp.stack([1.0 / (1.0 + jnp.exp(logit_gap)), 1.0 / (1.0 + jnp.exp(-logit_gap))], axis=1)


def rotate(vectors, positions):
    half_dim = vectors.shape[-1] // 2
    inv_freq = jnp.exp(-math.log(10000.0) * jnp.arange(half_dim, dtype=jnp.float32) / half_dim)
    angles = positions[:, None] * inv_freq[None, :]
    cosine_table = jnp.cos(angles)
    sine_table = jnp.sin(angles)
    front_half = vectors[..., :half_dim]
    back_half = vectors[..., half_dim:]
    return jnp.concatenate(
        [
            front_half * cosine_table - back_half * sine_table,
            back_half * cosine_table + front_half * sine_table,
        ],
        axis=-1,
    )


def pick_length(lengths, wanted):
    return jnp.sum(jnp.where(jnp.arange(lengths.shape[0]) == wanted, lengths, 0))


def absorb(carry_state, queries, key_rows, value_rows, allowed):
    row_peak, row_total, row_accum = carry_state
    scale_factor = queries.shape[-1] ** (-0.5)
    scores = (
        jnp.einsum("hqd,hkd->hqk", queries, key_rows, preferred_element_type=jnp.float32)
        * scale_factor
    )
    scores = jnp.where(allowed[None], scores, NEG_LARGE)
    new_peak = jnp.maximum(row_peak, jnp.max(scores, axis=-1))
    weights = jnp.where(allowed[None], jnp.exp(scores - new_peak[..., None]), 0.0)
    shrink = jnp.exp(row_peak - new_peak)
    row_total = row_total * shrink + jnp.sum(weights, axis=-1)
    row_accum = row_accum * shrink[..., None] + jnp.einsum(
        "hqk,hkd->hqd", weights.astype(jnp.bfloat16), value_rows, preferred_element_type=jnp.float32
    )
    return (new_peak, row_total, row_accum)


def cache_pass(
    queries, source, lowest, highest, first_block, last_block, anchor, block_len, carry_state
):
    head_dim = source.shape[2] // 2

    def block_step(block_id, running):
        block_rows = lax.dynamic_slice_in_dim(source, block_id * block_len, block_len, 1)
        key_index = anchor + block_id * block_len + jnp.arange(block_len)
        allowed = ((key_index >= lowest) & (key_index < highest))[None, :]
        return absorb(
            running, queries, block_rows[..., :head_dim], block_rows[..., head_dim:], allowed
        )

    return lax.fori_loop(
        jnp.asarray(first_block, jnp.int32),
        jnp.asarray(last_block, jnp.int32),
        block_step,
        carry_state,
    )


def chain_reduce(parts, axis):
    count = lax.axis_size(axis)
    me = lax.axis_index(axis)
    blocks = parts.reshape(count, parts.shape[0] // count, parts.shape[1])
    own = lax.dynamic_index_in_dim(blocks, me, 0, keepdims=False).astype(jnp.float32)
    if count == 1:
        return own.astype(parts.dtype)

    def run(step_block, pairs_of):
        received = None
        for step in range(1, count):
            block = lax.dynamic_index_in_dim(
                blocks, jnp.clip(step_block(step), 0, count - 1), 0, keepdims=False
            )
            if received is not None:
                block = (received.astype(jnp.float32) + block.astype(jnp.float32)).astype(
                    parts.dtype
                )
            received = lax.ppermute(block, axis, pairs_of(step))
        return received.astype(jnp.float32)

    rightward = run(
        lambda step: me + count - step,
        lambda step: [(src, src + 1) for src in range(step) if src + 1 < count],
    )
    leftward = run(
        lambda step: me - count + step,
        lambda step: [(src, src - 1) for src in range(count - step, count) if src >= 1],
    )
    return (own + rightward + leftward).astype(parts.dtype)


def exchange_parts(rows, weight, axis):
    count = lax.axis_size(axis)
    me = lax.axis_index(axis)
    span = rows.shape[0] // count
    parts = []
    for shift in list(range(1, count)) + [0]:
        target = lax.rem(me + shift, count)
        block_rows = lax.dynamic_slice_in_dim(rows, target * span, span, 0)
        product = jnp.einsum("tk,rkc->trc", block_rows, weight, preferred_element_type=jnp.float32)
        parts.append(product.reshape(span, -1).astype(jnp.bfloat16))
    return parts


def exchange_finish(parts, axis):
    count = lax.axis_size(axis)
    total = parts[-1].astype(jnp.float32)
    for shift, part in zip(range(1, count), parts):
        moved = lax.ppermute(part, axis, [(src, (src + shift) % count) for src in range(count)])
        total = total + moved.astype(jnp.float32)
    return total.astype(jnp.bfloat16)

def attention_kernel(
    length_ref, q_ref, cache_ref, fresh_ref, out_ref, peak_ref, total_ref, accum_ref, *, cache_blocks
):
    q_block = pl.program_id(1)
    kv_block = pl.program_id(2)
    rows, head_dim = q_ref.shape
    span = cache_ref.shape[1]
    length = length_ref[0]

    @pl.when(kv_block == 0)
    def _():
        peak_ref[...] = jnp.full(peak_ref.shape, NEG_LARGE, jnp.float32)
        total_ref[...] = jnp.zeros(total_ref.shape, jnp.float32)
        accum_ref[...] = jnp.zeros(accum_ref.shape, jnp.float32)

    def absorb_block(block, allowed):
        queries = q_ref[...]
        scores = lax.dot_general(
            queries,
            block[:, :head_dim],
            (((1,), (1,)), ((), ())),
            preferred_element_type=jnp.float32,
        ) * (head_dim ** (-0.5))
        scores = jnp.where(allowed, scores, NEG_LARGE)
        old_peak = peak_ref[...]
        new_peak = jnp.maximum(old_peak, jnp.max(scores, axis=-1, keepdims=True))
        weights = jnp.where(allowed, jnp.exp(scores - new_peak), 0.0)
        shrink = jnp.exp(old_peak - new_peak)
        total_ref[...] = total_ref[...] * shrink + jnp.sum(weights, axis=-1, keepdims=True)
        accum_ref[...] = accum_ref[...] * shrink + jnp.dot(
            weights.astype(jnp.bfloat16), block[:, head_dim:], preferred_element_type=jnp.float32
        )
        peak_ref[...] = new_peak

    @pl.when((kv_block < cache_blocks) & (kv_block * span < length))
    def _():
        key_index = kv_block * span + lax.broadcasted_iota(jnp.int32, (1, span), 1)
        absorb_block(cache_ref[0], key_index < length)

    @pl.when(kv_block == cache_blocks)
    def _():
        row_token = (q_block * rows + lax.broadcasted_iota(jnp.int32, (rows, 1), 0)) % span
        key_index = lax.broadcasted_iota(jnp.int32, (1, span), 1)
        absorb_block(fresh_ref[0], key_index <= row_token)
        out_ref[...] = accum_ref[...] / total_ref[...]


def attend(queries, cache, fresh, length):
    heads, span, head_dim = fresh.shape[0], fresh.shape[1], fresh.shape[2] // 2
    query_rows = queries.shape[0]
    cache_blocks = cache.shape[1] // span
    rows = min(query_rows, 512)

    def cache_map(h, i, j, length_ref):
        last = jnp.maximum((length_ref[0] + span - 1) // span - 1, 0)
        return (h, jnp.minimum(j, last), 0)

    grid_spec = pltpu.PrefetchScalarGridSpec(
        num_scalar_prefetch=1,
        grid=(heads, query_rows // rows, cache_blocks + 1),
        in_specs=[
            pl.BlockSpec((rows, head_dim), lambda h, i, j, length_ref: (i, h)),
            pl.BlockSpec((1, span, 2 * head_dim), cache_map),
            pl.BlockSpec((1, span, 2 * head_dim), lambda h, i, j, length_ref: (h, 0, 0)),
        ],
        out_specs=pl.BlockSpec((rows, head_dim), lambda h, i, j, length_ref: (i, h)),
        scratch_shapes=[
            pltpu.VMEM((rows, 1), jnp.float32),
            pltpu.VMEM((rows, 1), jnp.float32),
            pltpu.VMEM((rows, head_dim), jnp.float32),
        ],
    )
    keys_seen = 4 * heads * query_rows * (cache.shape[1] + span) * head_dim
    return pl.pallas_call(
        functools.partial(attention_kernel, cache_blocks=cache_blocks),
        out_shape=jax.ShapeDtypeStruct(queries.shape, jnp.float32),
        grid_spec=grid_spec,
        compiler_params=pltpu.CompilerParams(
            dimension_semantics=("arbitrary", "arbitrary", "arbitrary")
        ),
        cost_estimate=pl.CostEstimate(
            flops=keys_seen,
            transcendentals=heads * query_rows * (cache.shape[1] + span),
            bytes_accessed=2 * (cache.size + fresh.size + queries.size) + 4 * queries.size,
        ),
    )(jnp.reshape(length, (1,)).astype(jnp.int32), queries, cache, fresh)


def shards(
    tokens,
    norm_gain,
    router_weight,
    kv_weight,
    query_weight,
    out_weight,
    expert_ids,
    lengths,
    kv_cache,
):
    normed = normalize(tokens, norm_gain)
    tok_count = normed.shape[0]
    experts = query_weight.shape[0]
    head_dim = kv_cache.shape[3] // 2
    local_heads = query_weight.shape[2] // head_dim
    cache_len = kv_cache.shape[2]
    block_len = min(512, cache_len // 4)
    gate_values = gate_pair(normed, router_weight, expert_ids)
    query_full = lax.all_gather(query_weight, "req", axis=1, tiled=True)
    query_full, kv_weight, out_weight = lax.optimization_barrier(
        (query_full, kv_weight, out_weight)
    )
    kv_full = lax.all_gather(kv_weight, "req", axis=0, tiled=True)
    half = out_weight.shape[2] // 2
    out_halves = [
        lax.all_gather(piece, "req", axis=0)
        for piece in (out_weight[:, :, :half], out_weight[:, :, half:])
    ]
    projected = jnp.dot(normed, kv_full, preferred_element_type=jnp.float32)
    query_all = jnp.einsum(
        "tc,ecn->etn", normed, query_full, preferred_element_type=jnp.float32
    )
    req_index = lax.axis_index("req")
    own_length = pick_length(lengths, req_index)
    positions = (own_length + jnp.arange(tok_count)).astype(jnp.float32)
    projected = projected.reshape(tok_count, local_heads, 2, head_dim)
    new_keys = rotate(jnp.transpose(projected[:, :, 0], (1, 0, 2)), positions)
    new_values = jnp.transpose(projected[:, :, 1], (1, 0, 2))
    fresh_kv = jnp.concatenate([new_keys, new_values], axis=-1).astype(jnp.bfloat16)
    one_hot = jnp.arange(experts)[None, None, :] == expert_ids[:, :, None]
    choice_hot = jnp.transpose(one_hot, (1, 2, 0))
    query_sel = jnp.sum(jnp.where(choice_hot[..., None], query_all[None], 0.0), axis=1)
    query_sel = query_sel.reshape(2, tok_count, local_heads, head_dim)
    queries = rotate(query_sel, positions[:, None]).astype(jnp.bfloat16)
    queries = queries.reshape(2 * tok_count, local_heads * head_dim)
    heads_out = attend(queries, kv_cache[0], fresh_kv, own_length)
    heads_out = heads_out.reshape(2, tok_count, local_heads * head_dim)
    weighted = (jnp.transpose(gate_values)[:, :, None] * heads_out).astype(jnp.bfloat16)
    token_hot = jnp.transpose(one_hot, (1, 0, 2))
    mixture = jnp.sum(jnp.where(token_hot[..., None], weighted[:, :, None, :], 0), axis=0)
    mixture_flat = mixture.reshape(tok_count, experts * local_heads * head_dim)
    flat_halves = [
        piece.reshape(piece.shape[0], experts * local_heads * head_dim, piece.shape[3])
        for piece in out_halves
    ]
    first_parts = exchange_parts(mixture_flat, flat_halves[0], "head")
    _, second_weight = lax.optimization_barrier((first_parts, flat_halves[1]))
    results = [
        exchange_finish(first_parts, "head"),
        exchange_finish(exchange_parts(mixture_flat, second_weight, "head"), "head"),
    ]
    column_blocks = out_halves[0].shape[0]
    result = jnp.stack(
        [part.reshape(part.shape[0], column_blocks, half) for part in results], axis=2
    ).reshape(results[0].shape[0], 2 * half * column_blocks)
    return (result, fresh_kv[None])


def solution(mesh):
    placed = (
        P("req", None),
        P(),
        P(),
        P("req", "head"),
        P(None, "req", "head"),
        P(None, "head", "req"),
        P("req", None),
        P(),
        P("req", "head", None, None),
    )
    return jax.shard_map(
        shards,
        mesh=mesh,
        in_specs=placed,
        out_specs=(P(("req", "head"), None), P("req", "head", None, None)),
        check_vma=False,
    )
```

```python
import functools
import math

import jax
import jax.numpy as jnp
from jax import lax
from jax.experimental import pallas as pl
from jax.experimental.pallas import tpu as pltpu
from jax.sharding import PartitionSpec as P

NEG_LARGE = -1e30
EPSILON = 1e-06


def normalize(tokens, norm_gain):
    widened = tokens.astype(jnp.float32)
    factor = lax.rsqrt(jnp.mean(widened * widened, axis=-1, keepdims=True) + EPSILON)
    return (widened * factor * norm_gain).astype(jnp.bfloat16)


def gate_pair(normed, router_weight, expert_ids):
    logits = jnp.dot(normed.astype(jnp.float32), router_weight, precision=lax.Precision.HIGHEST)
    one_hot = jnp.arange(router_weight.shape[1])[None, None, :] == expert_ids[:, :, None]
    chosen = jnp.sum(jnp.where(one_hot, logits[:, None, :], 0.0), axis=-1)
    logit_gap = chosen[:, 1] - chosen[:, 0]
    return jnp.stack([1.0 / (1.0 + jnp.exp(logit_gap)), 1.0 / (1.0 + jnp.exp(-logit_gap))], axis=1)


def rotate(vectors, positions):
    half_dim = vectors.shape[-1] // 2
    inv_freq = jnp.exp(-math.log(10000.0) * jnp.arange(half_dim, dtype=jnp.float32) / half_dim)
    angles = positions[:, None] * inv_freq[None, :]
    cosine_table = jnp.cos(angles)
    sine_table = jnp.sin(angles)
    front_half = vectors[..., :half_dim]
    back_half = vectors[..., half_dim:]
    return jnp.concatenate(
        [
            front_half * cosine_table - back_half * sine_table,
            back_half * cosine_table + front_half * sine_table,
        ],
        axis=-1,
    )


def pick_length(lengths, wanted):
    return jnp.sum(jnp.where(jnp.arange(lengths.shape[0]) == wanted, lengths, 0))


def absorb(carry_state, queries, key_rows, value_rows, allowed):
    row_peak, row_total, row_accum = carry_state
    scale_factor = queries.shape[-1] ** (-0.5)
    scores = (
        jnp.einsum("hqd,hkd->hqk", queries, key_rows, preferred_element_type=jnp.float32)
        * scale_factor
    )
    scores = jnp.where(allowed[None], scores, NEG_LARGE)
    new_peak = jnp.maximum(row_peak, jnp.max(scores, axis=-1))
    weights = jnp.where(allowed[None], jnp.exp(scores - new_peak[..., None]), 0.0)
    shrink = jnp.exp(row_peak - new_peak)
    row_total = row_total * shrink + jnp.sum(weights, axis=-1)
    row_accum = row_accum * shrink[..., None] + jnp.einsum(
        "hqk,hkd->hqd", weights.astype(jnp.bfloat16), value_rows, preferred_element_type=jnp.float32
    )
    return (new_peak, row_total, row_accum)


def cache_pass(
    queries, source, lowest, highest, first_block, last_block, anchor, block_len, carry_state
):
    head_dim = source.shape[2] // 2

    def block_step(block_id, running):
        block_rows = lax.dynamic_slice_in_dim(source, block_id * block_len, block_len, 1)
        key_index = anchor + block_id * block_len + jnp.arange(block_len)
        allowed = ((key_index >= lowest) & (key_index < highest))[None, :]
        return absorb(
            running, queries, block_rows[..., :head_dim], block_rows[..., head_dim:], allowed
        )

    return lax.fori_loop(
        jnp.asarray(first_block, jnp.int32),
        jnp.asarray(last_block, jnp.int32),
        block_step,
        carry_state,
    )


def chain_reduce(parts, axis):
    count = lax.axis_size(axis)
    me = lax.axis_index(axis)
    blocks = parts.reshape(count, parts.shape[0] // count, parts.shape[1])
    own = lax.dynamic_index_in_dim(blocks, me, 0, keepdims=False).astype(jnp.float32)
    if count == 1:
        return own.astype(parts.dtype)

    def run(step_block, pairs_of):
        received = None
        for step in range(1, count):
            block = lax.dynamic_index_in_dim(
                blocks, jnp.clip(step_block(step), 0, count - 1), 0, keepdims=False
            )
            if received is not None:
                block = (received.astype(jnp.float32) + block.astype(jnp.float32)).astype(
                    parts.dtype
                )
            received = lax.ppermute(block, axis, pairs_of(step))
        return received.astype(jnp.float32)

    rightward = run(
        lambda step: me + count - step,
        lambda step: [(src, src + 1) for src in range(step) if src + 1 < count],
    )
    leftward = run(
        lambda step: me - count + step,
        lambda step: [(src, src - 1) for src in range(count - step, count) if src >= 1],
    )
    return (own + rightward + leftward).astype(parts.dtype)


def exchange_parts(rows, weight, axis):
    count = lax.axis_size(axis)
    me = lax.axis_index(axis)
    span = rows.shape[0] // count
    parts = []
    for shift in list(range(1, count)) + [0]:
        target = lax.rem(me + shift, count)
        block_rows = lax.dynamic_slice_in_dim(rows, target * span, span, 0)
        parts.append(
            jnp.dot(block_rows, weight, preferred_element_type=jnp.float32).astype(jnp.bfloat16)
        )
    return parts


def exchange_finish(parts, axis):
    count = lax.axis_size(axis)
    total = parts[-1].astype(jnp.float32)
    for shift, part in zip(range(1, count), parts):
        moved = lax.ppermute(part, axis, [(src, (src + shift) % count) for src in range(count)])
        total = total + moved.astype(jnp.float32)
    return total.astype(jnp.bfloat16)

def attention_kernel(
    length_ref, q_ref, cache_ref, fresh_ref, out_ref, peak_ref, total_ref, accum_ref, *, cache_blocks
):
    q_block = pl.program_id(1)
    kv_block = pl.program_id(2)
    rows, head_dim = q_ref.shape
    span = cache_ref.shape[1]
    length = length_ref[0]

    @pl.when(kv_block == 0)
    def _():
        peak_ref[...] = jnp.full(peak_ref.shape, NEG_LARGE, jnp.float32)
        total_ref[...] = jnp.zeros(total_ref.shape, jnp.float32)
        accum_ref[...] = jnp.zeros(accum_ref.shape, jnp.float32)

    def absorb_block(block, allowed):
        queries = q_ref[...]
        scores = lax.dot_general(
            queries,
            block[:, :head_dim],
            (((1,), (1,)), ((), ())),
            preferred_element_type=jnp.float32,
        ) * (head_dim ** (-0.5))
        if allowed is not None:
            scores = jnp.where(allowed, scores, NEG_LARGE)
        old_peak = peak_ref[...]
        new_peak = jnp.maximum(old_peak, jnp.max(scores, axis=-1, keepdims=True))
        weights = jnp.exp(scores - new_peak)
        if allowed is not None:
            weights = jnp.where(allowed, weights, 0.0)
        shrink = jnp.exp(old_peak - new_peak)
        total_ref[...] = total_ref[...] * shrink + jnp.sum(weights, axis=-1, keepdims=True)
        accum_ref[...] = accum_ref[...] * shrink + jnp.dot(
            weights.astype(jnp.bfloat16), block[:, head_dim:], preferred_element_type=jnp.float32
        )
        peak_ref[...] = new_peak

    @pl.when((kv_block < cache_blocks) & ((kv_block + 1) * span <= length))
    def _():
        absorb_block(cache_ref[0], None)

    @pl.when((kv_block < cache_blocks) & (kv_block * span < length) & ((kv_block + 1) * span > length))
    def _():
        key_index = kv_block * span + lax.broadcasted_iota(jnp.int32, (1, span), 1)
        absorb_block(cache_ref[0], key_index < length)

    @pl.when(kv_block == cache_blocks)
    def _():
        row_token = (q_block * rows + lax.broadcasted_iota(jnp.int32, (rows, 1), 0)) % span
        key_index = lax.broadcasted_iota(jnp.int32, (1, span), 1)
        absorb_block(fresh_ref[0], key_index <= row_token)
        out_ref[...] = accum_ref[...] / total_ref[...]


def attend(queries, cache, fresh, length):
    heads, span, head_dim = fresh.shape[0], fresh.shape[1], fresh.shape[2] // 2
    query_rows = queries.shape[0]
    cache_blocks = cache.shape[1] // span
    rows = min(query_rows, 512)

    def cache_map(h, i, j, length_ref):
        last = jnp.maximum((length_ref[0] + span - 1) // span - 1, 0)
        return (h, jnp.minimum(j, last), 0)

    grid_spec = pltpu.PrefetchScalarGridSpec(
        num_scalar_prefetch=1,
        grid=(heads, query_rows // rows, cache_blocks + 1),
        in_specs=[
            pl.BlockSpec((rows, head_dim), lambda h, i, j, length_ref: (i, h)),
            pl.BlockSpec((1, span, 2 * head_dim), cache_map),
            pl.BlockSpec((1, span, 2 * head_dim), lambda h, i, j, length_ref: (h, 0, 0)),
        ],
        out_specs=pl.BlockSpec((rows, head_dim), lambda h, i, j, length_ref: (i, h)),
        scratch_shapes=[
            pltpu.VMEM((rows, 1), jnp.float32),
            pltpu.VMEM((rows, 1), jnp.float32),
            pltpu.VMEM((rows, head_dim), jnp.float32),
        ],
    )
    keys_seen = 4 * heads * query_rows * (cache.shape[1] + span) * head_dim
    return pl.pallas_call(
        functools.partial(attention_kernel, cache_blocks=cache_blocks),
        out_shape=jax.ShapeDtypeStruct(queries.shape, jnp.float32),
        grid_spec=grid_spec,
        compiler_params=pltpu.CompilerParams(
            dimension_semantics=("arbitrary", "arbitrary", "arbitrary")
        ),
        cost_estimate=pl.CostEstimate(
            flops=keys_seen,
            transcendentals=heads * query_rows * (cache.shape[1] + span),
            bytes_accessed=2 * (cache.size + fresh.size + queries.size) + 4 * queries.size,
        ),
    )(jnp.reshape(length, (1,)).astype(jnp.int32), queries, cache, fresh)


def shards(
    tokens,
    norm_gain,
    router_weight,
    kv_weight,
    query_weight,
    out_weight,
    expert_ids,
    lengths,
    kv_cache,
):
    normed = normalize(tokens, norm_gain)
    tok_count = normed.shape[0]
    experts = query_weight.shape[0]
    head_dim = kv_cache.shape[3] // 2
    local_heads = query_weight.shape[2] // head_dim
    cache_len = kv_cache.shape[2]
    block_len = min(512, cache_len // 4)
    gate_values = gate_pair(normed, router_weight, expert_ids)
    depth, kv_width = kv_weight.shape
    query_local = jnp.transpose(query_weight, (1, 0, 2)).reshape(depth, -1)
    both_full = lax.all_gather(
        jnp.concatenate([query_local, kv_weight], axis=1), "req", axis=0, tiled=True
    )
    both_full, out_weight = lax.optimization_barrier((both_full, out_weight))
    query_full = both_full[:, : query_local.shape[1]].reshape(
        both_full.shape[0], query_weight.shape[0], query_weight.shape[2]
    )
    kv_full = both_full[:, query_local.shape[1] :]
    half = out_weight.shape[2] // 2
    out_halves = [
        lax.all_gather(piece, "req", axis=2, tiled=True)
        for piece in (out_weight[:, :, :half], out_weight[:, :, half:])
    ]
    projected = jnp.dot(normed, kv_full, preferred_element_type=jnp.float32)
    query_all = jnp.einsum(
        "tc,cen->etn", normed, query_full, preferred_element_type=jnp.float32
    )
    req_index = lax.axis_index("req")
    own_length = pick_length(lengths, req_index)
    positions = (own_length + jnp.arange(tok_count)).astype(jnp.float32)
    projected = projected.reshape(tok_count, local_heads, 2, head_dim)
    new_keys = rotate(jnp.transpose(projected[:, :, 0], (1, 0, 2)), positions)
    new_values = jnp.transpose(projected[:, :, 1], (1, 0, 2))
    fresh_kv = jnp.concatenate([new_keys, new_values], axis=-1).astype(jnp.bfloat16)
    one_hot = jnp.arange(experts)[None, None, :] == expert_ids[:, :, None]
    choice_hot = jnp.transpose(one_hot, (1, 2, 0))
    query_sel = jnp.sum(jnp.where(choice_hot[..., None], query_all[None], 0.0), axis=1)
    query_sel = query_sel.reshape(2, tok_count, local_heads, head_dim)
    queries = rotate(query_sel, positions[:, None]).astype(jnp.bfloat16)
    queries = queries.reshape(2 * tok_count, local_heads * head_dim)
    heads_out = attend(queries, kv_cache[0], fresh_kv, own_length)
    heads_out = heads_out.reshape(2, tok_count, local_heads * head_dim)
    weighted = (jnp.transpose(gate_values)[:, :, None] * heads_out).astype(jnp.bfloat16)
    token_hot = jnp.transpose(one_hot, (1, 0, 2))
    mixture = jnp.sum(jnp.where(token_hot[..., None], weighted[:, :, None, :], 0), axis=0)
    mixture_flat = mixture.reshape(tok_count, experts * local_heads * head_dim)
    flat_halves = [
        piece.reshape(experts * local_heads * head_dim, piece.shape[2]) for piece in out_halves
    ]
    first_parts = exchange_parts(mixture_flat, flat_halves[0], "head")
    _, second_weight = lax.optimization_barrier((first_parts, flat_halves[1]))
    results = [
        exchange_finish(first_parts, "head"),
        exchange_finish(exchange_parts(mixture_flat, second_weight, "head"), "head"),
    ]
    column_blocks = out_halves[0].shape[2] // half
    result = jnp.stack(
        [part.reshape(part.shape[0], column_blocks, half) for part in results], axis=2
    ).reshape(results[0].shape[0], 2 * half * column_blocks)
    return (result, fresh_kv[None])


def solution(mesh):
    placed = (
        P("req", None),
        P(),
        P(),
        P("req", "head"),
        P(None, "req", "head"),
        P(None, "head", "req"),
        P("req", None),
        P(),
        P("req", "head", None, None),
    )
    return jax.shard_map(
        shards,
        mesh=mesh,
        in_specs=placed,
        out_specs=(P(("req", "head"), None), P("req", "head", None, None)),
        check_vma=False,
    )
```

```python
import functools
import math

import jax
import jax.numpy as jnp
from jax import lax
from jax.experimental import pallas as pl
from jax.experimental.pallas import tpu as pltpu
from jax.sharding import PartitionSpec as P

NEG_LARGE = -1e30
EPSILON = 1e-06


def normalize(tokens, norm_gain):
    widened = tokens.astype(jnp.float32)
    factor = lax.rsqrt(jnp.mean(widened * widened, axis=-1, keepdims=True) + EPSILON)
    return (widened * factor * norm_gain).astype(jnp.bfloat16)


def gate_pair(normed, router_weight, expert_ids):
    logits = jnp.dot(normed.astype(jnp.float32), router_weight, precision=lax.Precision.HIGHEST)
    one_hot = jnp.arange(router_weight.shape[1])[None, None, :] == expert_ids[:, :, None]
    chosen = jnp.sum(jnp.where(one_hot, logits[:, None, :], 0.0), axis=-1)
    logit_gap = chosen[:, 1] - chosen[:, 0]
    return jnp.stack([1.0 / (1.0 + jnp.exp(logit_gap)), 1.0 / (1.0 + jnp.exp(-logit_gap))], axis=1)


def rotate(vectors, positions):
    half_dim = vectors.shape[-1] // 2
    inv_freq = jnp.exp(-math.log(10000.0) * jnp.arange(half_dim, dtype=jnp.float32) / half_dim)
    angles = positions[:, None] * inv_freq[None, :]
    cosine_table = jnp.cos(angles)
    sine_table = jnp.sin(angles)
    front_half = vectors[..., :half_dim]
    back_half = vectors[..., half_dim:]
    return jnp.concatenate(
        [
            front_half * cosine_table - back_half * sine_table,
            back_half * cosine_table + front_half * sine_table,
        ],
        axis=-1,
    )


def pick_length(lengths, wanted):
    return jnp.sum(jnp.where(jnp.arange(lengths.shape[0]) == wanted, lengths, 0))


def absorb(carry_state, queries, key_rows, value_rows, allowed):
    row_peak, row_total, row_accum = carry_state
    scale_factor = queries.shape[-1] ** (-0.5)
    scores = (
        jnp.einsum("hqd,hkd->hqk", queries, key_rows, preferred_element_type=jnp.float32)
        * scale_factor
    )
    scores = jnp.where(allowed[None], scores, NEG_LARGE)
    new_peak = jnp.maximum(row_peak, jnp.max(scores, axis=-1))
    weights = jnp.where(allowed[None], jnp.exp(scores - new_peak[..., None]), 0.0)
    shrink = jnp.exp(row_peak - new_peak)
    row_total = row_total * shrink + jnp.sum(weights, axis=-1)
    row_accum = row_accum * shrink[..., None] + jnp.einsum(
        "hqk,hkd->hqd", weights.astype(jnp.bfloat16), value_rows, preferred_element_type=jnp.float32
    )
    return (new_peak, row_total, row_accum)


def cache_pass(
    queries, source, lowest, highest, first_block, last_block, anchor, block_len, carry_state
):
    head_dim = source.shape[2] // 2

    def block_step(block_id, running):
        block_rows = lax.dynamic_slice_in_dim(source, block_id * block_len, block_len, 1)
        key_index = anchor + block_id * block_len + jnp.arange(block_len)
        allowed = ((key_index >= lowest) & (key_index < highest))[None, :]
        return absorb(
            running, queries, block_rows[..., :head_dim], block_rows[..., head_dim:], allowed
        )

    return lax.fori_loop(
        jnp.asarray(first_block, jnp.int32),
        jnp.asarray(last_block, jnp.int32),
        block_step,
        carry_state,
    )


def chain_reduce(parts, axis):
    count = lax.axis_size(axis)
    me = lax.axis_index(axis)
    blocks = parts.reshape(count, parts.shape[0] // count, parts.shape[1])
    own = lax.dynamic_index_in_dim(blocks, me, 0, keepdims=False).astype(jnp.float32)
    if count == 1:
        return own.astype(parts.dtype)

    def run(step_block, pairs_of):
        received = None
        for step in range(1, count):
            block = lax.dynamic_index_in_dim(
                blocks, jnp.clip(step_block(step), 0, count - 1), 0, keepdims=False
            )
            if received is not None:
                block = (received.astype(jnp.float32) + block.astype(jnp.float32)).astype(
                    parts.dtype
                )
            received = lax.ppermute(block, axis, pairs_of(step))
        return received.astype(jnp.float32)

    rightward = run(
        lambda step: me + count - step,
        lambda step: [(src, src + 1) for src in range(step) if src + 1 < count],
    )
    leftward = run(
        lambda step: me - count + step,
        lambda step: [(src, src - 1) for src in range(count - step, count) if src >= 1],
    )
    return (own + rightward + leftward).astype(parts.dtype)


def exchange_parts(rows, weight, axis):
    count = lax.axis_size(axis)
    me = lax.axis_index(axis)
    span = rows.shape[0] // count
    parts = []
    for shift in list(range(1, count)) + [0]:
        target = lax.rem(me + shift, count)
        block_rows = lax.dynamic_slice_in_dim(rows, target * span, span, 0)
        parts.append(
            jnp.dot(block_rows, weight, preferred_element_type=jnp.float32).astype(jnp.bfloat16)
        )
    return parts


def exchange_finish(parts, axis):
    count = lax.axis_size(axis)
    total = parts[-1].astype(jnp.float32)
    for shift, part in zip(range(1, count), parts):
        moved = lax.ppermute(part, axis, [(src, (src + shift) % count) for src in range(count)])
        total = total + moved.astype(jnp.float32)
    return total.astype(jnp.bfloat16)

def attention_kernel(
    length_ref, q_ref, cache_ref, fresh_ref, out_ref, peak_ref, total_ref, accum_ref, *, cache_blocks
):
    q_block = pl.program_id(1)
    kv_block = pl.program_id(2)
    rows, head_dim = q_ref.shape
    span = cache_ref.shape[1]
    length = length_ref[0]

    @pl.when(kv_block == 0)
    def _():
        peak_ref[...] = jnp.full(peak_ref.shape, NEG_LARGE, jnp.float32)
        total_ref[...] = jnp.zeros(total_ref.shape, jnp.float32)
        accum_ref[...] = jnp.zeros(accum_ref.shape, jnp.float32)

    def absorb_block(block, allowed):
        queries = q_ref[...]
        scores = lax.dot_general(
            queries,
            block[:, :head_dim],
            (((1,), (1,)), ((), ())),
            preferred_element_type=jnp.float32,
        ) * (head_dim ** (-0.5))
        scores = jnp.where(allowed, scores, NEG_LARGE)
        old_peak = peak_ref[...]
        new_peak = jnp.maximum(old_peak, jnp.max(scores, axis=-1, keepdims=True))
        weights = jnp.where(allowed, jnp.exp(scores - new_peak), 0.0)
        shrink = jnp.exp(old_peak - new_peak)
        total_ref[...] = total_ref[...] * shrink + jnp.sum(weights, axis=-1, keepdims=True)
        accum_ref[...] = accum_ref[...] * shrink + jnp.dot(
            weights.astype(jnp.bfloat16), block[:, head_dim:], preferred_element_type=jnp.float32
        )
        peak_ref[...] = new_peak

    @pl.when((kv_block < cache_blocks) & (kv_block * span < length))
    def _():
        key_index = kv_block * span + lax.broadcasted_iota(jnp.int32, (1, span), 1)
        absorb_block(cache_ref[0], key_index < length)

    @pl.when(kv_block == cache_blocks)
    def _():
        row_token = (q_block * rows + lax.broadcasted_iota(jnp.int32, (rows, 1), 0)) % span
        key_index = lax.broadcasted_iota(jnp.int32, (1, span), 1)
        absorb_block(fresh_ref[0], key_index <= row_token)
        out_ref[...] = accum_ref[...] / total_ref[...]


def attend(queries, cache, fresh, length):
    heads, span, head_dim = fresh.shape[0], fresh.shape[1], fresh.shape[2] // 2
    query_rows = queries.shape[0]
    cache_blocks = cache.shape[1] // span
    rows = min(query_rows, 1024)

    def cache_map(h, i, j, length_ref):
        last = jnp.maximum((length_ref[0] + span - 1) // span - 1, 0)
        return (h, jnp.minimum(j, last), 0)

    grid_spec = pltpu.PrefetchScalarGridSpec(
        num_scalar_prefetch=1,
        grid=(heads, query_rows // rows, cache_blocks + 1),
        in_specs=[
            pl.BlockSpec((rows, head_dim), lambda h, i, j, length_ref: (i, h)),
            pl.BlockSpec((1, span, 2 * head_dim), cache_map),
            pl.BlockSpec((1, span, 2 * head_dim), lambda h, i, j, length_ref: (h, 0, 0)),
        ],
        out_specs=pl.BlockSpec((rows, head_dim), lambda h, i, j, length_ref: (i, h)),
        scratch_shapes=[
            pltpu.VMEM((rows, 1), jnp.float32),
            pltpu.VMEM((rows, 1), jnp.float32),
            pltpu.VMEM((rows, head_dim), jnp.float32),
        ],
    )
    keys_seen = 4 * heads * query_rows * (cache.shape[1] + span) * head_dim
    return pl.pallas_call(
        functools.partial(attention_kernel, cache_blocks=cache_blocks),
        out_shape=jax.ShapeDtypeStruct(queries.shape, jnp.float32),
        grid_spec=grid_spec,
        compiler_params=pltpu.CompilerParams(
            dimension_semantics=("arbitrary", "arbitrary", "arbitrary")
        ),
        cost_estimate=pl.CostEstimate(
            flops=keys_seen,
            transcendentals=heads * query_rows * (cache.shape[1] + span),
            bytes_accessed=2 * (cache.size + fresh.size + queries.size) + 4 * queries.size,
        ),
    )(jnp.reshape(length, (1,)).astype(jnp.int32), queries, cache, fresh)


def shards(
    tokens,
    norm_gain,
    router_weight,
    kv_weight,
    query_weight,
    out_weight,
    expert_ids,
    lengths,
    kv_cache,
):
    normed = normalize(tokens, norm_gain)
    tok_count = normed.shape[0]
    experts = query_weight.shape[0]
    head_dim = kv_cache.shape[3] // 2
    local_heads = query_weight.shape[2] // head_dim
    cache_len = kv_cache.shape[2]
    block_len = min(512, cache_len // 4)
    gate_values = gate_pair(normed, router_weight, expert_ids)
    query_full = lax.all_gather(query_weight, "req", axis=1, tiled=True)
    query_full, kv_weight, out_weight = lax.optimization_barrier(
        (query_full, kv_weight, out_weight)
    )
    kv_full = lax.all_gather(kv_weight, "req", axis=0, tiled=True)
    half = out_weight.shape[2] // 2
    out_halves = [
        lax.all_gather(piece, "req", axis=2, tiled=True)
        for piece in (out_weight[:, :, :half], out_weight[:, :, half:])
    ]
    projected = jnp.dot(normed, kv_full, preferred_element_type=jnp.float32)
    query_all = jnp.einsum(
        "tc,ecn->etn", normed, query_full, preferred_element_type=jnp.float32
    )
    req_index = lax.axis_index("req")
    own_length = pick_length(lengths, req_index)
    positions = (own_length + jnp.arange(tok_count)).astype(jnp.float32)
    projected = projected.reshape(tok_count, local_heads, 2, head_dim)
    new_keys = rotate(jnp.transpose(projected[:, :, 0], (1, 0, 2)), positions)
    new_values = jnp.transpose(projected[:, :, 1], (1, 0, 2))
    fresh_kv = jnp.concatenate([new_keys, new_values], axis=-1).astype(jnp.bfloat16)
    one_hot = jnp.arange(experts)[None, None, :] == expert_ids[:, :, None]
    choice_hot = jnp.transpose(one_hot, (1, 2, 0))
    query_sel = jnp.sum(jnp.where(choice_hot[..., None], query_all[None], 0.0), axis=1)
    query_sel = query_sel.reshape(2, tok_count, local_heads, head_dim)
    queries = rotate(query_sel, positions[:, None]).astype(jnp.bfloat16)
    queries = queries.reshape(2 * tok_count, local_heads * head_dim)
    heads_out = attend(queries, kv_cache[0], fresh_kv, own_length)
    heads_out = heads_out.reshape(2, tok_count, local_heads * head_dim)
    weighted = (jnp.transpose(gate_values)[:, :, None] * heads_out).astype(jnp.bfloat16)
    token_hot = jnp.transpose(one_hot, (1, 0, 2))
    mixture = jnp.sum(jnp.where(token_hot[..., None], weighted[:, :, None, :], 0), axis=0)
    mixture_flat = mixture.reshape(tok_count, experts * local_heads * head_dim)
    flat_halves = [
        piece.reshape(experts * local_heads * head_dim, piece.shape[2]) for piece in out_halves
    ]
    first_parts = exchange_parts(mixture_flat, flat_halves[0], "head")
    _, second_weight = lax.optimization_barrier((first_parts, flat_halves[1]))
    results = [
        exchange_finish(first_parts, "head"),
        exchange_finish(exchange_parts(mixture_flat, second_weight, "head"), "head"),
    ]
    column_blocks = out_halves[0].shape[2] // half
    result = jnp.stack(
        [part.reshape(part.shape[0], column_blocks, half) for part in results], axis=2
    ).reshape(results[0].shape[0], 2 * half * column_blocks)
    return (result, fresh_kv[None])


def solution(mesh):
    placed = (
        P("req", None),
        P(),
        P(),
        P("req", "head"),
        P(None, "req", "head"),
        P(None, "head", "req"),
        P("req", None),
        P(),
        P("req", "head", None, None),
    )
    return jax.shard_map(
        shards,
        mesh=mesh,
        in_specs=placed,
        out_specs=(P(("req", "head"), None), P("req", "head", None, None)),
        check_vma=False,
    )
```

```python
import functools
import math

import jax
import jax.numpy as jnp
from jax import lax
from jax.experimental import pallas as pl
from jax.experimental.pallas import tpu as pltpu
from jax.sharding import PartitionSpec as P

NEG_LARGE = -1e30
EPSILON = 1e-06


def normalize(tokens, norm_gain):
    widened = tokens.astype(jnp.float32)
    factor = lax.rsqrt(jnp.mean(widened * widened, axis=-1, keepdims=True) + EPSILON)
    return (widened * factor * norm_gain).astype(jnp.bfloat16)


def gate_pair(normed, router_weight, expert_ids):
    logits = jnp.dot(normed.astype(jnp.float32), router_weight, precision=lax.Precision.HIGHEST)
    one_hot = jnp.arange(router_weight.shape[1])[None, None, :] == expert_ids[:, :, None]
    chosen = jnp.sum(jnp.where(one_hot, logits[:, None, :], 0.0), axis=-1)
    logit_gap = chosen[:, 1] - chosen[:, 0]
    return jnp.stack([1.0 / (1.0 + jnp.exp(logit_gap)), 1.0 / (1.0 + jnp.exp(-logit_gap))], axis=1)


def rotate(vectors, positions):
    half_dim = vectors.shape[-1] // 2
    inv_freq = jnp.exp(-math.log(10000.0) * jnp.arange(half_dim, dtype=jnp.float32) / half_dim)
    angles = positions[:, None] * inv_freq[None, :]
    cosine_table = jnp.cos(angles)
    sine_table = jnp.sin(angles)
    front_half = vectors[..., :half_dim]
    back_half = vectors[..., half_dim:]
    return jnp.concatenate(
        [
            front_half * cosine_table - back_half * sine_table,
            back_half * cosine_table + front_half * sine_table,
        ],
        axis=-1,
    )


def pick_length(lengths, wanted):
    return jnp.sum(jnp.where(jnp.arange(lengths.shape[0]) == wanted, lengths, 0))


def absorb(carry_state, queries, key_rows, value_rows, allowed):
    row_peak, row_total, row_accum = carry_state
    scale_factor = queries.shape[-1] ** (-0.5)
    scores = (
        jnp.einsum("hqd,hkd->hqk", queries, key_rows, preferred_element_type=jnp.float32)
        * scale_factor
    )
    scores = jnp.where(allowed[None], scores, NEG_LARGE)
    new_peak = jnp.maximum(row_peak, jnp.max(scores, axis=-1))
    weights = jnp.where(allowed[None], jnp.exp(scores - new_peak[..., None]), 0.0)
    shrink = jnp.exp(row_peak - new_peak)
    row_total = row_total * shrink + jnp.sum(weights, axis=-1)
    row_accum = row_accum * shrink[..., None] + jnp.einsum(
        "hqk,hkd->hqd", weights.astype(jnp.bfloat16), value_rows, preferred_element_type=jnp.float32
    )
    return (new_peak, row_total, row_accum)


def cache_pass(
    queries, source, lowest, highest, first_block, last_block, anchor, block_len, carry_state
):
    head_dim = source.shape[2] // 2

    def block_step(block_id, running):
        block_rows = lax.dynamic_slice_in_dim(source, block_id * block_len, block_len, 1)
        key_index = anchor + block_id * block_len + jnp.arange(block_len)
        allowed = ((key_index >= lowest) & (key_index < highest))[None, :]
        return absorb(
            running, queries, block_rows[..., :head_dim], block_rows[..., head_dim:], allowed
        )

    return lax.fori_loop(
        jnp.asarray(first_block, jnp.int32),
        jnp.asarray(last_block, jnp.int32),
        block_step,
        carry_state,
    )


def chain_reduce(parts, axis):
    count = lax.axis_size(axis)
    me = lax.axis_index(axis)
    blocks = parts.reshape(count, parts.shape[0] // count, parts.shape[1])
    own = lax.dynamic_index_in_dim(blocks, me, 0, keepdims=False).astype(jnp.float32)
    if count == 1:
        return own.astype(parts.dtype)

    def run(step_block, pairs_of):
        received = None
        for step in range(1, count):
            block = lax.dynamic_index_in_dim(
                blocks, jnp.clip(step_block(step), 0, count - 1), 0, keepdims=False
            )
            if received is not None:
                block = (received.astype(jnp.float32) + block.astype(jnp.float32)).astype(
                    parts.dtype
                )
            received = lax.ppermute(block, axis, pairs_of(step))
        return received.astype(jnp.float32)

    rightward = run(
        lambda step: me + count - step,
        lambda step: [(src, src + 1) for src in range(step) if src + 1 < count],
    )
    leftward = run(
        lambda step: me - count + step,
        lambda step: [(src, src - 1) for src in range(count - step, count) if src >= 1],
    )
    return (own + rightward + leftward).astype(parts.dtype)


def exchange_parts(rows, weight, axis):
    count = lax.axis_size(axis)
    me = lax.axis_index(axis)
    span = rows.shape[0] // count
    parts = []
    for shift in list(range(1, count)) + [0]:
        target = lax.rem(me + shift, count)
        block_rows = lax.dynamic_slice_in_dim(rows, target * span, span, 0)
        parts.append(
            jnp.dot(block_rows, weight, preferred_element_type=jnp.float32).astype(jnp.bfloat16)
        )
    return parts


def exchange_finish(parts, axis):
    count = lax.axis_size(axis)
    total = parts[-1].astype(jnp.float32)
    for shift, part in zip(range(1, count), parts):
        moved = lax.ppermute(part, axis, [(src, (src + shift) % count) for src in range(count)])
        total = total + moved.astype(jnp.float32)
    return total.astype(jnp.bfloat16)

def attention_kernel(
    length_ref, q_ref, cache_ref, fresh_ref, out_ref, peak_ref, total_ref, accum_ref, *, cache_blocks
):
    q_block = pl.program_id(1)
    kv_block = pl.program_id(2)
    rows, head_dim = q_ref.shape
    span = cache_ref.shape[1]
    length = length_ref[0]

    @pl.when(kv_block == 0)
    def _():
        peak_ref[...] = jnp.full(peak_ref.shape, NEG_LARGE, jnp.float32)
        total_ref[...] = jnp.zeros(total_ref.shape, jnp.float32)
        accum_ref[...] = jnp.zeros(accum_ref.shape, jnp.float32)

    def absorb_block(block, allowed):
        queries = q_ref[...]
        scores = lax.dot_general(
            queries,
            block[:, :head_dim],
            (((1,), (1,)), ((), ())),
            preferred_element_type=jnp.float32,
        ) * (head_dim ** (-0.5))
        scores = jnp.where(allowed, scores, NEG_LARGE)
        old_peak = peak_ref[...]
        new_peak = jnp.maximum(old_peak, jnp.max(scores, axis=-1, keepdims=True))
        weights = jnp.where(allowed, jnp.exp(scores - new_peak), 0.0)
        shrink = jnp.exp(old_peak - new_peak)
        total_ref[...] = total_ref[...] * shrink + jnp.sum(weights, axis=-1, keepdims=True)
        accum_ref[...] = accum_ref[...] * shrink + jnp.dot(
            weights.astype(jnp.bfloat16), block[:, head_dim:], preferred_element_type=jnp.float32
        )
        peak_ref[...] = new_peak

    @pl.when((kv_block < cache_blocks) & (kv_block * span < length))
    def _():
        key_index = kv_block * span + lax.broadcasted_iota(jnp.int32, (1, span), 1)
        absorb_block(cache_ref[0], key_index < length)

    @pl.when(kv_block == cache_blocks)
    def _():
        row_token = (q_block * rows + lax.broadcasted_iota(jnp.int32, (rows, 1), 0)) % span
        key_index = lax.broadcasted_iota(jnp.int32, (1, span), 1)
        absorb_block(fresh_ref[0], key_index <= row_token)
        out_ref[...] = accum_ref[...] / total_ref[...]


def attend(queries, cache, fresh, length):
    heads, span, head_dim = fresh.shape[0], fresh.shape[1], fresh.shape[2] // 2
    query_rows = queries.shape[0]
    cache_blocks = cache.shape[1] // span
    rows = min(query_rows, 512)

    def cache_map(h, i, j, length_ref):
        last = jnp.maximum((length_ref[0] + span - 1) // span - 1, 0)
        return (h, jnp.minimum(j, last), 0)

    grid_spec = pltpu.PrefetchScalarGridSpec(
        num_scalar_prefetch=1,
        grid=(heads, query_rows // rows, cache_blocks + 1),
        in_specs=[
            pl.BlockSpec((rows, head_dim), lambda h, i, j, length_ref: (i, h)),
            pl.BlockSpec((1, span, 2 * head_dim), cache_map),
            pl.BlockSpec((1, span, 2 * head_dim), lambda h, i, j, length_ref: (h, 0, 0)),
        ],
        out_specs=pl.BlockSpec((rows, head_dim), lambda h, i, j, length_ref: (i, h)),
        scratch_shapes=[
            pltpu.VMEM((rows, 1), jnp.float32),
            pltpu.VMEM((rows, 1), jnp.float32),
            pltpu.VMEM((rows, head_dim), jnp.float32),
        ],
    )
    keys_seen = 4 * heads * query_rows * (cache.shape[1] + span) * head_dim
    return pl.pallas_call(
        functools.partial(attention_kernel, cache_blocks=cache_blocks),
        out_shape=jax.ShapeDtypeStruct(queries.shape, jnp.float32),
        grid_spec=grid_spec,
        compiler_params=pltpu.CompilerParams(
            dimension_semantics=("arbitrary", "arbitrary", "arbitrary")
        ),
        cost_estimate=pl.CostEstimate(
            flops=keys_seen,
            transcendentals=heads * query_rows * (cache.shape[1] + span),
            bytes_accessed=2 * (cache.size + fresh.size + queries.size) + 4 * queries.size,
        ),
    )(jnp.reshape(length, (1,)).astype(jnp.int32), queries, cache, fresh)


def xor_gather(block, axis):
    count = lax.axis_size(axis)
    me = lax.axis_index(axis)
    if count & (count - 1):
        return lax.all_gather(block, axis, axis=0, tiled=True)
    arrived = [block] + [
        lax.ppermute(block, axis, [(src, src ^ step) for src in range(count)])
        for step in range(1, count)
    ]
    order = jnp.bitwise_xor(me, jnp.arange(count))
    stacked = jnp.take(jnp.stack(arrived), order, axis=0)
    return stacked.reshape(count * block.shape[0], *block.shape[1:])


def shards(
    tokens,
    norm_gain,
    router_weight,
    kv_weight,
    query_weight,
    out_weight,
    expert_ids,
    lengths,
    kv_cache,
):
    normed = normalize(tokens, norm_gain)
    tok_count = normed.shape[0]
    experts = query_weight.shape[0]
    head_dim = kv_cache.shape[3] // 2
    local_heads = query_weight.shape[2] // head_dim
    cache_len = kv_cache.shape[2]
    block_len = min(512, cache_len // 4)
    gate_values = gate_pair(normed, router_weight, expert_ids)
    query_full = lax.all_gather(query_weight, "req", axis=1, tiled=True)
    query_full, kv_weight, out_weight = lax.optimization_barrier(
        (query_full, kv_weight, out_weight)
    )
    kv_full = xor_gather(kv_weight, "req")
    half = out_weight.shape[2] // 2
    out_halves = [
        lax.all_gather(piece, "req", axis=2, tiled=True)
        for piece in (out_weight[:, :, :half], out_weight[:, :, half:])
    ]
    projected = jnp.dot(normed, kv_full, preferred_element_type=jnp.float32)
    query_all = jnp.einsum(
        "tc,ecn->etn", normed, query_full, preferred_element_type=jnp.float32
    )
    req_index = lax.axis_index("req")
    own_length = pick_length(lengths, req_index)
    positions = (own_length + jnp.arange(tok_count)).astype(jnp.float32)
    projected = projected.reshape(tok_count, local_heads, 2, head_dim)
    new_keys = rotate(jnp.transpose(projected[:, :, 0], (1, 0, 2)), positions)
    new_values = jnp.transpose(projected[:, :, 1], (1, 0, 2))
    fresh_kv = jnp.concatenate([new_keys, new_values], axis=-1).astype(jnp.bfloat16)
    one_hot = jnp.arange(experts)[None, None, :] == expert_ids[:, :, None]
    choice_hot = jnp.transpose(one_hot, (1, 2, 0))
    query_sel = jnp.sum(jnp.where(choice_hot[..., None], query_all[None], 0.0), axis=1)
    query_sel = query_sel.reshape(2, tok_count, local_heads, head_dim)
    queries = rotate(query_sel, positions[:, None]).astype(jnp.bfloat16)
    queries = queries.reshape(2 * tok_count, local_heads * head_dim)
    heads_out = attend(queries, kv_cache[0], fresh_kv, own_length)
    heads_out = heads_out.reshape(2, tok_count, local_heads * head_dim)
    weighted = (jnp.transpose(gate_values)[:, :, None] * heads_out).astype(jnp.bfloat16)
    token_hot = jnp.transpose(one_hot, (1, 0, 2))
    mixture = jnp.sum(jnp.where(token_hot[..., None], weighted[:, :, None, :], 0), axis=0)
    mixture_flat = mixture.reshape(tok_count, experts * local_heads * head_dim)
    flat_halves = [
        piece.reshape(experts * local_heads * head_dim, piece.shape[2]) for piece in out_halves
    ]
    first_parts = exchange_parts(mixture_flat, flat_halves[0], "head")
    _, second_weight = lax.optimization_barrier((first_parts, flat_halves[1]))
    results = [
        exchange_finish(first_parts, "head"),
        exchange_finish(exchange_parts(mixture_flat, second_weight, "head"), "head"),
    ]
    column_blocks = out_halves[0].shape[2] // half
    result = jnp.stack(
        [part.reshape(part.shape[0], column_blocks, half) for part in results], axis=2
    ).reshape(results[0].shape[0], 2 * half * column_blocks)
    return (result, fresh_kv[None])


def solution(mesh):
    placed = (
        P("req", None),
        P(),
        P(),
        P("req", "head"),
        P(None, "req", "head"),
        P(None, "head", "req"),
        P("req", None),
        P(),
        P("req", "head", None, None),
    )
    return jax.shard_map(
        shards,
        mesh=mesh,
        in_specs=placed,
        out_specs=(P(("req", "head"), None), P("req", "head", None, None)),
        check_vma=False,
    )
```

```python
import functools
import math

import jax
import jax.numpy as jnp
from jax import lax
from jax.experimental import pallas as pl
from jax.experimental.pallas import tpu as pltpu
from jax.sharding import PartitionSpec as P

NEG_LARGE = -1e30
EPSILON = 1e-06


def normalize(tokens, norm_gain):
    widened = tokens.astype(jnp.float32)
    factor = lax.rsqrt(jnp.mean(widened * widened, axis=-1, keepdims=True) + EPSILON)
    return (widened * factor * norm_gain).astype(jnp.bfloat16)


def gate_pair(normed, router_weight, expert_ids):
    logits = jnp.dot(normed.astype(jnp.float32), router_weight, precision=lax.Precision.HIGHEST)
    one_hot = jnp.arange(router_weight.shape[1])[None, None, :] == expert_ids[:, :, None]
    chosen = jnp.sum(jnp.where(one_hot, logits[:, None, :], 0.0), axis=-1)
    logit_gap = chosen[:, 1] - chosen[:, 0]
    return jnp.stack([1.0 / (1.0 + jnp.exp(logit_gap)), 1.0 / (1.0 + jnp.exp(-logit_gap))], axis=1)


def rotate(vectors, positions):
    half_dim = vectors.shape[-1] // 2
    inv_freq = jnp.exp(-math.log(10000.0) * jnp.arange(half_dim, dtype=jnp.float32) / half_dim)
    angles = positions[:, None] * inv_freq[None, :]
    cosine_table = jnp.cos(angles)
    sine_table = jnp.sin(angles)
    front_half = vectors[..., :half_dim]
    back_half = vectors[..., half_dim:]
    return jnp.concatenate(
        [
            front_half * cosine_table - back_half * sine_table,
            back_half * cosine_table + front_half * sine_table,
        ],
        axis=-1,
    )


def pick_length(lengths, wanted):
    return jnp.sum(jnp.where(jnp.arange(lengths.shape[0]) == wanted, lengths, 0))


def absorb(carry_state, queries, key_rows, value_rows, allowed):
    row_peak, row_total, row_accum = carry_state
    scale_factor = queries.shape[-1] ** (-0.5)
    scores = (
        jnp.einsum("hqd,hkd->hqk", queries, key_rows, preferred_element_type=jnp.float32)
        * scale_factor
    )
    scores = jnp.where(allowed[None], scores, NEG_LARGE)
    new_peak = jnp.maximum(row_peak, jnp.max(scores, axis=-1))
    weights = jnp.where(allowed[None], jnp.exp(scores - new_peak[..., None]), 0.0)
    shrink = jnp.exp(row_peak - new_peak)
    row_total = row_total * shrink + jnp.sum(weights, axis=-1)
    row_accum = row_accum * shrink[..., None] + jnp.einsum(
        "hqk,hkd->hqd", weights.astype(jnp.bfloat16), value_rows, preferred_element_type=jnp.float32
    )
    return (new_peak, row_total, row_accum)


def cache_pass(
    queries, source, lowest, highest, first_block, last_block, anchor, block_len, carry_state
):
    head_dim = source.shape[2] // 2

    def block_step(block_id, running):
        block_rows = lax.dynamic_slice_in_dim(source, block_id * block_len, block_len, 1)
        key_index = anchor + block_id * block_len + jnp.arange(block_len)
        allowed = ((key_index >= lowest) & (key_index < highest))[None, :]
        return absorb(
            running, queries, block_rows[..., :head_dim], block_rows[..., head_dim:], allowed
        )

    return lax.fori_loop(
        jnp.asarray(first_block, jnp.int32),
        jnp.asarray(last_block, jnp.int32),
        block_step,
        carry_state,
    )


def chain_reduce(parts, axis):
    count = lax.axis_size(axis)
    me = lax.axis_index(axis)
    blocks = parts.reshape(count, parts.shape[0] // count, parts.shape[1])
    own = lax.dynamic_index_in_dim(blocks, me, 0, keepdims=False).astype(jnp.float32)
    if count == 1:
        return own.astype(parts.dtype)

    def run(step_block, pairs_of):
        received = None
        for step in range(1, count):
            block = lax.dynamic_index_in_dim(
                blocks, jnp.clip(step_block(step), 0, count - 1), 0, keepdims=False
            )
            if received is not None:
                block = (received.astype(jnp.float32) + block.astype(jnp.float32)).astype(
                    parts.dtype
                )
            received = lax.ppermute(block, axis, pairs_of(step))
        return received.astype(jnp.float32)

    rightward = run(
        lambda step: me + count - step,
        lambda step: [(src, src + 1) for src in range(step) if src + 1 < count],
    )
    leftward = run(
        lambda step: me - count + step,
        lambda step: [(src, src - 1) for src in range(count - step, count) if src >= 1],
    )
    return (own + rightward + leftward).astype(parts.dtype)


def exchange_parts(rows, weight, axis):
    count = lax.axis_size(axis)
    me = lax.axis_index(axis)
    span = rows.shape[0] // count
    parts = []
    for shift in list(range(1, count)) + [0]:
        if not shift:
            parts, rows = lax.optimization_barrier((parts, rows))
        target = lax.rem(me + shift, count)
        block_rows = lax.dynamic_slice_in_dim(rows, target * span, span, 0)
        parts.append(
            jnp.dot(block_rows, weight, preferred_element_type=jnp.float32).astype(jnp.bfloat16)
        )
    return parts


def exchange_finish(parts, axis):
    count = lax.axis_size(axis)
    total = parts[-1].astype(jnp.float32)
    for shift, part in zip(range(1, count), parts):
        moved = lax.ppermute(part, axis, [(src, (src + shift) % count) for src in range(count)])
        total = total + moved.astype(jnp.float32)
    return total.astype(jnp.bfloat16)

def attention_kernel(
    length_ref, q_ref, cache_ref, fresh_ref, out_ref, peak_ref, total_ref, accum_ref, *, cache_blocks
):
    q_block = pl.program_id(1)
    kv_block = pl.program_id(2)
    rows, head_dim = q_ref.shape
    span = cache_ref.shape[1]
    length = length_ref[0]

    @pl.when(kv_block == 0)
    def _():
        peak_ref[...] = jnp.full(peak_ref.shape, NEG_LARGE, jnp.float32)
        total_ref[...] = jnp.zeros(total_ref.shape, jnp.float32)
        accum_ref[...] = jnp.zeros(accum_ref.shape, jnp.float32)

    def absorb_block(block, allowed):
        queries = q_ref[...]
        scores = lax.dot_general(
            queries,
            block[:, :head_dim],
            (((1,), (1,)), ((), ())),
            preferred_element_type=jnp.float32,
        ) * (head_dim ** (-0.5))
        scores = jnp.where(allowed, scores, NEG_LARGE)
        old_peak = peak_ref[...]
        new_peak = jnp.maximum(old_peak, jnp.max(scores, axis=-1, keepdims=True))
        weights = jnp.where(allowed, jnp.exp(scores - new_peak), 0.0)
        shrink = jnp.exp(old_peak - new_peak)
        total_ref[...] = total_ref[...] * shrink + jnp.sum(weights, axis=-1, keepdims=True)
        accum_ref[...] = accum_ref[...] * shrink + jnp.dot(
            weights.astype(jnp.bfloat16), block[:, head_dim:], preferred_element_type=jnp.float32
        )
        peak_ref[...] = new_peak

    @pl.when((kv_block < cache_blocks) & (kv_block * span < length))
    def _():
        key_index = kv_block * span + lax.broadcasted_iota(jnp.int32, (1, span), 1)
        absorb_block(cache_ref[0], key_index < length)

    @pl.when(kv_block == cache_blocks)
    def _():
        row_token = (q_block * rows + lax.broadcasted_iota(jnp.int32, (rows, 1), 0)) % span
        key_index = lax.broadcasted_iota(jnp.int32, (1, span), 1)
        absorb_block(fresh_ref[0], key_index <= row_token)
        out_ref[...] = accum_ref[...] / total_ref[...]


def attend(queries, cache, fresh, length):
    heads, span, head_dim = fresh.shape[0], fresh.shape[1], fresh.shape[2] // 2
    query_rows = queries.shape[0]
    cache_blocks = cache.shape[1] // span
    rows = min(query_rows, 512)

    def cache_map(h, i, j, length_ref):
        last = jnp.maximum((length_ref[0] + span - 1) // span - 1, 0)
        return (h, jnp.minimum(j, last), 0)

    grid_spec = pltpu.PrefetchScalarGridSpec(
        num_scalar_prefetch=1,
        grid=(heads, query_rows // rows, cache_blocks + 1),
        in_specs=[
            pl.BlockSpec((rows, head_dim), lambda h, i, j, length_ref: (i, h)),
            pl.BlockSpec((1, span, 2 * head_dim), cache_map),
            pl.BlockSpec((1, span, 2 * head_dim), lambda h, i, j, length_ref: (h, 0, 0)),
        ],
        out_specs=pl.BlockSpec((rows, head_dim), lambda h, i, j, length_ref: (i, h)),
        scratch_shapes=[
            pltpu.VMEM((rows, 1), jnp.float32),
            pltpu.VMEM((rows, 1), jnp.float32),
            pltpu.VMEM((rows, head_dim), jnp.float32),
        ],
    )
    keys_seen = 4 * heads * query_rows * (cache.shape[1] + span) * head_dim
    return pl.pallas_call(
        functools.partial(attention_kernel, cache_blocks=cache_blocks),
        out_shape=jax.ShapeDtypeStruct(queries.shape, jnp.float32),
        grid_spec=grid_spec,
        compiler_params=pltpu.CompilerParams(
            dimension_semantics=("arbitrary", "arbitrary", "arbitrary")
        ),
        cost_estimate=pl.CostEstimate(
            flops=keys_seen,
            transcendentals=heads * query_rows * (cache.shape[1] + span),
            bytes_accessed=2 * (cache.size + fresh.size + queries.size) + 4 * queries.size,
        ),
    )(jnp.reshape(length, (1,)).astype(jnp.int32), queries, cache, fresh)


def shards(
    tokens,
    norm_gain,
    router_weight,
    kv_weight,
    query_weight,
    out_weight,
    expert_ids,
    lengths,
    kv_cache,
):
    normed = normalize(tokens, norm_gain)
    tok_count = normed.shape[0]
    experts = query_weight.shape[0]
    head_dim = kv_cache.shape[3] // 2
    local_heads = query_weight.shape[2] // head_dim
    cache_len = kv_cache.shape[2]
    block_len = min(512, cache_len // 4)
    gate_values = gate_pair(normed, router_weight, expert_ids)
    query_full = lax.all_gather(query_weight, "req", axis=1, tiled=True)
    query_full, kv_weight, out_weight = lax.optimization_barrier(
        (query_full, kv_weight, out_weight)
    )
    kv_full = lax.all_gather(kv_weight, "req", axis=0, tiled=True)
    half = out_weight.shape[2] // 2
    out_halves = [
        lax.all_gather(piece, "req", axis=2, tiled=True)
        for piece in (out_weight[:, :, :half], out_weight[:, :, half:])
    ]
    projected = jnp.dot(normed, kv_full, preferred_element_type=jnp.float32)
    query_all = jnp.einsum(
        "tc,ecn->etn", normed, query_full, preferred_element_type=jnp.float32
    )
    req_index = lax.axis_index("req")
    own_length = pick_length(lengths, req_index)
    positions = (own_length + jnp.arange(tok_count)).astype(jnp.float32)
    projected = projected.reshape(tok_count, local_heads, 2, head_dim)
    new_keys = rotate(jnp.transpose(projected[:, :, 0], (1, 0, 2)), positions)
    new_values = jnp.transpose(projected[:, :, 1], (1, 0, 2))
    fresh_kv = jnp.concatenate([new_keys, new_values], axis=-1).astype(jnp.bfloat16)
    one_hot = jnp.arange(experts)[None, None, :] == expert_ids[:, :, None]
    choice_hot = jnp.transpose(one_hot, (1, 2, 0))
    query_sel = jnp.sum(jnp.where(choice_hot[..., None], query_all[None], 0.0), axis=1)
    query_sel = query_sel.reshape(2, tok_count, local_heads, head_dim)
    queries = rotate(query_sel, positions[:, None]).astype(jnp.bfloat16)
    queries = queries.reshape(2 * tok_count, local_heads * head_dim)
    heads_out = attend(queries, kv_cache[0], fresh_kv, own_length)
    heads_out = heads_out.reshape(2, tok_count, local_heads * head_dim)
    weighted = (jnp.transpose(gate_values)[:, :, None] * heads_out).astype(jnp.bfloat16)
    token_hot = jnp.transpose(one_hot, (1, 0, 2))
    mixture = jnp.sum(jnp.where(token_hot[..., None], weighted[:, :, None, :], 0), axis=0)
    mixture_flat = mixture.reshape(tok_count, experts * local_heads * head_dim)
    flat_halves = [
        piece.reshape(experts * local_heads * head_dim, piece.shape[2]) for piece in out_halves
    ]
    first_parts = exchange_parts(mixture_flat, flat_halves[0], "head")
    _, second_weight = lax.optimization_barrier((first_parts, flat_halves[1]))
    results = [
        exchange_finish(first_parts, "head"),
        exchange_finish(exchange_parts(mixture_flat, second_weight, "head"), "head"),
    ]
    column_blocks = out_halves[0].shape[2] // half
    result = jnp.stack(
        [part.reshape(part.shape[0], column_blocks, half) for part in results], axis=2
    ).reshape(results[0].shape[0], 2 * half * column_blocks)
    return (result, fresh_kv[None])


def solution(mesh):
    placed = (
        P("req", None),
        P(),
        P(),
        P("req", "head"),
        P(None, "req", "head"),
        P(None, "head", "req"),
        P("req", None),
        P(),
        P("req", "head", None, None),
    )
    return jax.shard_map(
        shards,
        mesh=mesh,
        in_specs=placed,
        out_specs=(P(("req", "head"), None), P("req", "head", None, None)),
        check_vma=False,
    )
```

```python
import functools
import math

import jax
import jax.numpy as jnp
from jax import lax
from jax.experimental import pallas as pl
from jax.experimental.pallas import tpu as pltpu
from jax.sharding import PartitionSpec as P

NEG_LARGE = -1e30
EPSILON = 1e-06


def normalize(tokens, norm_gain):
    widened = tokens.astype(jnp.float32)
    factor = lax.rsqrt(jnp.mean(widened * widened, axis=-1, keepdims=True) + EPSILON)
    return (widened * factor * norm_gain).astype(jnp.bfloat16)


def gate_pair(normed, router_weight, expert_ids):
    logits = jnp.dot(normed.astype(jnp.float32), router_weight, precision=lax.Precision.HIGHEST)
    one_hot = jnp.arange(router_weight.shape[1])[None, None, :] == expert_ids[:, :, None]
    chosen = jnp.sum(jnp.where(one_hot, logits[:, None, :], 0.0), axis=-1)
    logit_gap = chosen[:, 1] - chosen[:, 0]
    return jnp.stack([1.0 / (1.0 + jnp.exp(logit_gap)), 1.0 / (1.0 + jnp.exp(-logit_gap))], axis=1)


def rotate(vectors, positions):
    half_dim = vectors.shape[-1] // 2
    inv_freq = jnp.exp(-math.log(10000.0) * jnp.arange(half_dim, dtype=jnp.float32) / half_dim)
    angles = positions[:, None] * inv_freq[None, :]
    cosine_table = jnp.cos(angles)
    sine_table = jnp.sin(angles)
    front_half = vectors[..., :half_dim]
    back_half = vectors[..., half_dim:]
    return jnp.concatenate(
        [
            front_half * cosine_table - back_half * sine_table,
            back_half * cosine_table + front_half * sine_table,
        ],
        axis=-1,
    )


def pick_length(lengths, wanted):
    return jnp.sum(jnp.where(jnp.arange(lengths.shape[0]) == wanted, lengths, 0))


def absorb(carry_state, queries, key_rows, value_rows, allowed):
    row_peak, row_total, row_accum = carry_state
    scale_factor = queries.shape[-1] ** (-0.5)
    scores = (
        jnp.einsum("hqd,hkd->hqk", queries, key_rows, preferred_element_type=jnp.float32)
        * scale_factor
    )
    scores = jnp.where(allowed[None], scores, NEG_LARGE)
    new_peak = jnp.maximum(row_peak, jnp.max(scores, axis=-1))
    weights = jnp.where(allowed[None], jnp.exp(scores - new_peak[..., None]), 0.0)
    shrink = jnp.exp(row_peak - new_peak)
    row_total = row_total * shrink + jnp.sum(weights, axis=-1)
    row_accum = row_accum * shrink[..., None] + jnp.einsum(
        "hqk,hkd->hqd", weights.astype(jnp.bfloat16), value_rows, preferred_element_type=jnp.float32
    )
    return (new_peak, row_total, row_accum)


def cache_pass(
    queries, source, lowest, highest, first_block, last_block, anchor, block_len, carry_state
):
    head_dim = source.shape[2] // 2

    def block_step(block_id, running):
        block_rows = lax.dynamic_slice_in_dim(source, block_id * block_len, block_len, 1)
        key_index = anchor + block_id * block_len + jnp.arange(block_len)
        allowed = ((key_index >= lowest) & (key_index < highest))[None, :]
        return absorb(
            running, queries, block_rows[..., :head_dim], block_rows[..., head_dim:], allowed
        )

    return lax.fori_loop(
        jnp.asarray(first_block, jnp.int32),
        jnp.asarray(last_block, jnp.int32),
        block_step,
        carry_state,
    )


def chain_reduce(parts, axis):
    count = lax.axis_size(axis)
    me = lax.axis_index(axis)
    blocks = parts.reshape(count, parts.shape[0] // count, parts.shape[1])
    own = lax.dynamic_index_in_dim(blocks, me, 0, keepdims=False).astype(jnp.float32)
    if count == 1:
        return own.astype(parts.dtype)

    def run(step_block, pairs_of):
        received = None
        for step in range(1, count):
            block = lax.dynamic_index_in_dim(
                blocks, jnp.clip(step_block(step), 0, count - 1), 0, keepdims=False
            )
            if received is not None:
                block = (received.astype(jnp.float32) + block.astype(jnp.float32)).astype(
                    parts.dtype
                )
            received = lax.ppermute(block, axis, pairs_of(step))
        return received.astype(jnp.float32)

    rightward = run(
        lambda step: me + count - step,
        lambda step: [(src, src + 1) for src in range(step) if src + 1 < count],
    )
    leftward = run(
        lambda step: me - count + step,
        lambda step: [(src, src - 1) for src in range(count - step, count) if src >= 1],
    )
    return (own + rightward + leftward).astype(parts.dtype)


def exchange_parts(rows, weight, axis):
    count = lax.axis_size(axis)
    me = lax.axis_index(axis)
    span = rows.shape[0] // count
    parts = []
    for shift in list(range(1, count)) + [0]:
        target = lax.rem(me + shift, count)
        block_rows = lax.dynamic_slice_in_dim(rows, target * span, span, 0)
        parts.append(
            jnp.dot(block_rows, weight, preferred_element_type=jnp.float32).astype(jnp.bfloat16)
        )
    return parts


def exchange_finish(parts, axis):
    count = lax.axis_size(axis)
    total = parts[-1].astype(jnp.float32)
    for shift, part in zip(range(1, count), parts):
        moved = lax.ppermute(part, axis, [(src, (src + shift) % count) for src in range(count)])
        total = total + moved.astype(jnp.float32)
    return total.astype(jnp.bfloat16)

def attention_kernel(
    length_ref, q_ref, cache_ref, fresh_ref, out_ref, peak_ref, total_ref, accum_ref, *, cache_blocks
):
    q_block = pl.program_id(1)
    kv_block = pl.program_id(2)
    rows, head_dim = q_ref.shape
    span = cache_ref.shape[1]
    length = length_ref[0]

    @pl.when(kv_block == 0)
    def _():
        peak_ref[...] = jnp.full(peak_ref.shape, NEG_LARGE, jnp.float32)
        total_ref[...] = jnp.zeros(total_ref.shape, jnp.float32)
        accum_ref[...] = jnp.zeros(accum_ref.shape, jnp.float32)

    def absorb_block(block, allowed):
        queries = q_ref[...]
        scores = lax.dot_general(
            queries,
            block[:, :head_dim],
            (((1,), (1,)), ((), ())),
            preferred_element_type=jnp.float32,
        ) * (head_dim ** (-0.5))
        scores = jnp.where(allowed, scores, NEG_LARGE)
        old_peak = peak_ref[...]
        new_peak = jnp.maximum(old_peak, jnp.max(scores, axis=-1, keepdims=True))
        weights = jnp.where(allowed, jnp.exp(scores - new_peak), 0.0)
        shrink = jnp.exp(old_peak - new_peak)
        total_ref[...] = total_ref[...] * shrink + jnp.sum(weights, axis=-1, keepdims=True)
        accum_ref[...] = accum_ref[...] * shrink + jnp.dot(
            weights.astype(jnp.bfloat16), block[:, head_dim:], preferred_element_type=jnp.float32
        )
        peak_ref[...] = new_peak

    @pl.when((kv_block < cache_blocks) & (kv_block * span < length))
    def _():
        key_index = kv_block * span + lax.broadcasted_iota(jnp.int32, (1, span), 1)
        absorb_block(cache_ref[0], key_index < length)

    @pl.when(kv_block == cache_blocks)
    def _():
        row_token = (q_block * rows + lax.broadcasted_iota(jnp.int32, (rows, 1), 0)) % span
        key_index = lax.broadcasted_iota(jnp.int32, (1, span), 1)
        absorb_block(fresh_ref[0], key_index <= row_token)
        out_ref[...] = accum_ref[...] / total_ref[...]


def attend(queries, cache, fresh, length):
    heads, span, head_dim = fresh.shape[0], fresh.shape[1], fresh.shape[2] // 2
    query_rows = queries.shape[0]
    cache_blocks = cache.shape[1] // span
    rows = min(query_rows, 256)

    def cache_map(h, i, j, length_ref):
        last = jnp.maximum((length_ref[0] + span - 1) // span - 1, 0)
        return (h, jnp.minimum(j, last), 0)

    grid_spec = pltpu.PrefetchScalarGridSpec(
        num_scalar_prefetch=1,
        grid=(heads, query_rows // rows, cache_blocks + 1),
        in_specs=[
            pl.BlockSpec((rows, head_dim), lambda h, i, j, length_ref: (i, h)),
            pl.BlockSpec((1, span, 2 * head_dim), cache_map),
            pl.BlockSpec((1, span, 2 * head_dim), lambda h, i, j, length_ref: (h, 0, 0)),
        ],
        out_specs=pl.BlockSpec((rows, head_dim), lambda h, i, j, length_ref: (i, h)),
        scratch_shapes=[
            pltpu.VMEM((rows, 1), jnp.float32),
            pltpu.VMEM((rows, 1), jnp.float32),
            pltpu.VMEM((rows, head_dim), jnp.float32),
        ],
    )
    keys_seen = 4 * heads * query_rows * (cache.shape[1] + span) * head_dim
    return pl.pallas_call(
        functools.partial(attention_kernel, cache_blocks=cache_blocks),
        out_shape=jax.ShapeDtypeStruct(queries.shape, jnp.float32),
        grid_spec=grid_spec,
        compiler_params=pltpu.CompilerParams(
            dimension_semantics=("arbitrary", "arbitrary", "arbitrary")
        ),
        cost_estimate=pl.CostEstimate(
            flops=keys_seen,
            transcendentals=heads * query_rows * (cache.shape[1] + span),
            bytes_accessed=2 * (cache.size + fresh.size + queries.size) + 4 * queries.size,
        ),
    )(jnp.reshape(length, (1,)).astype(jnp.int32), queries, cache, fresh)


def shards(
    tokens,
    norm_gain,
    router_weight,
    kv_weight,
    query_weight,
    out_weight,
    expert_ids,
    lengths,
    kv_cache,
):
    normed = normalize(tokens, norm_gain)
    tok_count = normed.shape[0]
    experts = query_weight.shape[0]
    head_dim = kv_cache.shape[3] // 2
    local_heads = query_weight.shape[2] // head_dim
    cache_len = kv_cache.shape[2]
    block_len = min(512, cache_len // 4)
    gate_values = gate_pair(normed, router_weight, expert_ids)
    query_full = lax.all_gather(query_weight, "req", axis=1, tiled=True)
    query_full, kv_weight, out_weight = lax.optimization_barrier(
        (query_full, kv_weight, out_weight)
    )
    kv_full = lax.all_gather(kv_weight, "req", axis=0, tiled=True)
    half = out_weight.shape[2] // 2
    out_halves = [
        lax.all_gather(piece, "req", axis=2, tiled=True)
        for piece in (out_weight[:, :, :half], out_weight[:, :, half:])
    ]
    projected = jnp.dot(normed, kv_full, preferred_element_type=jnp.float32)
    query_all = jnp.einsum(
        "tc,ecn->etn", normed, query_full, preferred_element_type=jnp.float32
    )
    req_index = lax.axis_index("req")
    own_length = pick_length(lengths, req_index)
    positions = (own_length + jnp.arange(tok_count)).astype(jnp.float32)
    projected = projected.reshape(tok_count, local_heads, 2, head_dim)
    new_keys = rotate(jnp.transpose(projected[:, :, 0], (1, 0, 2)), positions)
    new_values = jnp.transpose(projected[:, :, 1], (1, 0, 2))
    fresh_kv = jnp.concatenate([new_keys, new_values], axis=-1).astype(jnp.bfloat16)
    one_hot = jnp.arange(experts)[None, None, :] == expert_ids[:, :, None]
    choice_hot = jnp.transpose(one_hot, (1, 2, 0))
    query_sel = jnp.sum(jnp.where(choice_hot[..., None], query_all[None], 0.0), axis=1)
    query_sel = query_sel.reshape(2, tok_count, local_heads, head_dim)
    queries = rotate(query_sel, positions[:, None]).astype(jnp.bfloat16)
    queries = queries.reshape(2 * tok_count, local_heads * head_dim)
    heads_out = attend(queries, kv_cache[0], fresh_kv, own_length)
    heads_out = heads_out.reshape(2, tok_count, local_heads * head_dim)
    weighted = (jnp.transpose(gate_values)[:, :, None] * heads_out).astype(jnp.bfloat16)
    token_hot = jnp.transpose(one_hot, (1, 0, 2))
    mixture = jnp.sum(jnp.where(token_hot[..., None], weighted[:, :, None, :], 0), axis=0)
    mixture_flat = mixture.reshape(tok_count, experts * local_heads * head_dim)
    flat_halves = [
        piece.reshape(experts * local_heads * head_dim, piece.shape[2]) for piece in out_halves
    ]
    first_parts = exchange_parts(mixture_flat, flat_halves[0], "head")
    _, second_weight = lax.optimization_barrier((first_parts, flat_halves[1]))
    results = [
        exchange_finish(first_parts, "head"),
        exchange_finish(exchange_parts(mixture_flat, second_weight, "head"), "head"),
    ]
    column_blocks = out_halves[0].shape[2] // half
    result = jnp.stack(
        [part.reshape(part.shape[0], column_blocks, half) for part in results], axis=2
    ).reshape(results[0].shape[0], 2 * half * column_blocks)
    return (result, fresh_kv[None])


def solution(mesh):
    placed = (
        P("req", None),
        P(),
        P(),
        P("req", "head"),
        P(None, "req", "head"),
        P(None, "head", "req"),
        P("req", None),
        P(),
        P("req", "head", None, None),
    )
    return jax.shard_map(
        shards,
        mesh=mesh,
        in_specs=placed,
        out_specs=(P(("req", "head"), None), P("req", "head", None, None)),
        check_vma=False,
    )
```
